32 devices in a mesh: tm: 4 (over y, x), height: 2 (over core), chan: 4 (over z).
Axes of the slice: x: 2, y: 2, z: 4, core: 2. Of those that a mesh axis runs over, the one named last changes fastest.
Arguments:
- features: bfloat16 [384, 8, 8, 160], P('chan', 'tm', 'height'), may hold values from -400 to 400, as said below
- cotangent: bfloat16 [384, 8, 8, 160], P('chan', 'tm', 'height'), may hold values from -6 to 6
- conv_weight: bfloat16 [384, 27, 384], P('chan'), may hold values from -0.0625 to 0.0625
- norm_gain: float32 [384], replicated, may hold values from 0.5 to 1.5
- norm_bias: float32 [384], replicated, may hold values from -3 to 3
Outputs:
- input_grad: bfloat16 [384, 8, 8, 160], P('chan', 'tm', 'height')
- weight_grad: float32 [384, 27, 384], P('chan')
The draws below stay inside these ranges and needn't reach their ends.
Inputs may be any that keep to these rules, and one draw needn't show every extreme that they name: `features`: bounded activations.
All inputs are finite; a program needn't handle non-finite values.
Results may differ from the reference program's by a relative error of at most 0.003.
Values may be sent and summed in bfloat16 or wider, within the bound.
No kernel may reach another device: no remote copies, remote signals or barrier semaphores. Data moves between devices by JAX's collectives and lax.ppermute only.
A program may use at most 64 MiB of HBM per device.

```python
import math
import jax
import jax.numpy as jnp
from jax import lax

C = 384
WIDTH = 160
FRAMES = 8
ROWS_ALL = 8


def draw_features(key, part):
    k_chan, k_cell, k_base = jax.random.split(key, 3)
    lift = jnp.log(3.0)
    chan_index = jnp.arange(C, dtype=jnp.float32).reshape(C, 1, 1, 1)
    chan_scale = jnp.exp(jax.random.uniform(k_chan, (C, 1, 1, 1), jnp.float32, -1.2, 1.2) + lift * chan_index / C)
    row_index = jnp.arange(ROWS_ALL, dtype=jnp.float32).reshape(1, 1, ROWS_ALL, 1)
    cell_scale = jnp.exp(jax.random.uniform(k_cell, (1, FRAMES, ROWS_ALL, WIDTH), jnp.float32, -1.2, 1.2) + lift * row_index / ROWS_ALL)
    shape = (C, FRAMES, ROWS_ALL, WIDTH)
    base = jax.random.truncated_normal(k_base, -4.0, 4.0, shape, jnp.float32)
    return (base * chan_scale * cell_scale).astype(jnp.bfloat16)


def steps_of(own_key, dims, cuts, low, largest):
    gain, own = 1.0, jax.random.fold_in(own_key, 6)
    for axis_at, shards_of in cuts:
        draws = jnp.exp(jax.random.uniform(jax.random.fold_in(own, axis_at), (shards_of,), jnp.float32, low / len(cuts), largest / len(cuts)))
        gain = gain * jnp.repeat(draws, dims[axis_at] // shards_of).reshape([-1 if axis == axis_at else 1 for axis in range(len(dims))])
    return gain


def bell_draw(own_key, extent, width, most, shards=(), kind=jnp.bfloat16):
    values = width * jax.random.normal(own_key, extent, jnp.float32)
    if shards:
        values = values * steps_of(own_key, extent, shards, -0.22, 0.18)
    return jnp.clip(values, -most, most).astype(kind)


def setup_inputs(seed: int = 0) -> dict:
    seeds = jax.random.split(jax.random.key(seed), 6)
    return {
        "features": draw_features(jax.random.fold_in(seeds[5], 71), 0),
        "cotangent": bell_draw(seeds[1], (C, FRAMES, ROWS_ALL, WIDTH), 1.0, 6.0, ((0, 4), (1, 4), (2, 2))),
        "conv_weight": bell_draw(seeds[2], (C, 27, C), (27 * C) ** -0.5, 0.0625, ((0, 4),)),
        "norm_gain": jnp.clip(1.0 + 0.1 * jax.random.normal(seeds[3], (C,), jnp.float32), 0.5, 1.5),
        "norm_bias": bell_draw(seeds[4], (C,), 0.5, 3.0, (), jnp.float32),
    }


def reference(features, cotangent, conv_weight, norm_gain, norm_bias):
    total = features.shape[0]
    flat_x = features.reshape(total, -1).astype(jnp.float32)
    inv_rms = lax.rsqrt(lax.optimization_barrier(jnp.mean(flat_x * flat_x, axis=0, keepdims=True)) + 1e-06)
    normed = flat_x * inv_rms * norm_gain[:, None] + norm_bias[:, None]
    active = jax.nn.silu(normed).astype(jnp.bfloat16)
    frames, rows, cols = (features.shape[1], features.shape[2], features.shape[3])
    padded = jnp.pad(cotangent, ((0, 0), (0, 2), (1, 1), (1, 1)))
    act_grad = jnp.zeros(flat_x.shape, jnp.float32)
    pieces = []
    for kt in range(3):
        for kh in range(3):
            for kw in range(3):
                tapped = padded[:, 2 - kt:2 - kt + frames, 2 - kh:2 - kh + rows, 2 - kw:2 - kw + cols].reshape(total, -1)
                weight_tap = conv_weight[:, 9 * kt + 3 * kh + kw, :]
                act_grad = act_grad + lax.dot_general(weight_tap, tapped, (((0,), (0,)), ((), ())), preferred_element_type=jnp.float32)
                pieces.append(lax.dot_general(tapped, active, (((1,), (1,)), ((), ())), preferred_element_type=jnp.float32))
    weight_grad = jnp.stack(pieces, axis=1) / math.sqrt(flat_x.shape[1])
    sig = jax.nn.sigmoid(normed)
    upstream = act_grad * (sig * (1.0 + normed * (1.0 - sig))) * norm_gain[:, None]
    dots = lax.optimization_barrier(jnp.sum(upstream * flat_x, axis=0, keepdims=True))
    back = inv_rms * upstream - flat_x * inv_rms ** 3 * dots / total
    result = cotangent.reshape(total, -1).astype(jnp.float32) + back
    return (result.astype(jnp.bfloat16).reshape(features.shape), weight_grad)
```

```python
import math

import jax
import jax.numpy as jnp
from jax import lax
from jax.sharding import PartitionSpec as P


def from_behind(block, axis, distance):
    devices = range(lax.axis_size(axis))
    route = [(i - distance, i) for i in devices if i - distance in devices]
    return lax.ppermute(block, axis, route)


def with_halo(array, sides, width):
    for axis, dim in sides:
        size, length = (lax.axis_size(axis), array.shape[dim])
        up = [(i, (i + 1) % size) for i in range(size - 1)]
        down = [(j, i) for i, j in up]
        last = lax.slice_in_dim(array, length - width, length, axis=dim)
        first = lax.slice_in_dim(array, 0, width, axis=dim)
        before = lax.ppermute(last, axis, up)
        after = lax.ppermute(first, axis, down)
        array = jnp.concatenate([before, array, after], axis=dim)
    return array


def gather_blocks(block, axis):
    size = lax.axis_size(axis)
    me = lax.axis_index(axis)
    chans = block.shape[0]
    whole = jnp.zeros((chans * size,) + block.shape[1:], block.dtype)
    whole = lax.dynamic_update_slice_in_dim(whole, block, me * chans, axis=0)
    for d in range(1, size):
        got = lax.ppermute(block, axis, [(j, (j + d) % size) for j in range(size)])
        whole = lax.dynamic_update_slice_in_dim(
            whole, got, ((me - d) % size) * chans, axis=0
        )
    return whole


def reverse_space(array):
    return lax.rev(array, (1, 2, 3))


def on_device(features, cotangent, conv_weight, norm_gain, norm_bias):
    chans, frames, rows, cols = features.shape
    n_chan = lax.axis_size("chan")
    whole_x = gather_blocks(features, "chan")
    total = whole_x.shape[0]
    cells = frames * rows * cols
    flat_x = whole_x.reshape(total, cells).astype(jnp.float32)
    inv_rms = lax.rsqrt(jnp.mean(flat_x * flat_x, axis=0, keepdims=True) + 1e-06)
    normed = flat_x * inv_rms * norm_gain[:, None] + norm_bias[:, None]
    active = jax.nn.silu(normed).astype(jnp.bfloat16).reshape(total, frames, rows, cols)

    ahead = from_behind(lax.slice_in_dim(cotangent, 0, 2, axis=1), "tm", -1)
    longer = jnp.concatenate([cotangent, ahead], axis=1)
    bordered = with_halo(longer, (("height", 2),), 1)
    padded = jnp.pad(bordered, ((0, 0), (0, 0), (0, 0), (1, 1)))

    wdn = lax.ConvDimensionNumbers(
        lhs_spec=(1, 0, 2, 3, 4), rhs_spec=(1, 0, 2, 3, 4), out_spec=(0, 4, 1, 2, 3)
    )
    local_sums = lax.conv_general_dilated(
        reverse_space(padded)[None],
        reverse_space(active)[None],
        window_strides=(1, 1, 1),
        padding="VALID",
        dimension_numbers=wdn,
        preferred_element_type=jnp.float32,
    )
    positions = frames * lax.axis_size("tm") * rows * lax.axis_size("height") * cols
    summed = lax.psum(local_sums, ("tm", "height"))
    weight_grad = (summed / math.sqrt(positions)).reshape(chans, 27, total)

    kernel = conv_weight.reshape(chans, 3, 3, 3, total)
    kernel = lax.rev(kernel, (1, 2, 3))
    adn = lax.ConvDimensionNumbers(
        lhs_spec=(0, 1, 2, 3, 4), rhs_spec=(4, 0, 1, 2, 3), out_spec=(0, 1, 2, 3, 4)
    )
    partial = lax.conv_general_dilated(
        padded[None],
        kernel,
        window_strides=(1, 1, 1),
        padding="VALID",
        dimension_numbers=adn,
        preferred_element_type=jnp.float32,
    )[0].reshape(total, cells)

    sig = jax.nn.sigmoid(normed)
    slope = sig * (1.0 + normed * (1.0 - sig)) * norm_gain[:, None]
    part_dots = jnp.sum(partial * slope * flat_x, axis=0, keepdims=True)
    packed = jnp.concatenate(
        [
            partial.reshape(n_chan, chans, cells),
            jnp.broadcast_to(part_dots[None], (n_chan, 1, cells)),
        ],
        axis=1,
    )
    mine = lax.psum_scatter(packed, "chan", scatter_dimension=0, tiled=True)[0]
    act_grad = mine[:chans]
    dots = mine[chans:]

    offset = lax.axis_index("chan") * chans
    own_x = features.reshape(chans, -1).astype(jnp.float32)
    own_slope = lax.dynamic_slice_in_dim(slope, offset, chans, 0)
    upstream = act_grad * own_slope
    own_back = inv_rms * upstream - own_x * inv_rms**3 * dots / total
    result = cotangent.reshape(chans, -1).astype(jnp.float32) + own_back
    return (result.astype(jnp.bfloat16).reshape(features.shape), weight_grad)


def solution(mesh):
    return jax.shard_map(
        on_device,
        mesh=mesh,
        in_specs=(
            P("chan", "tm", "height", None),
            P("chan", "tm", "height", None),
            P("chan", None, None),
            P(),
            P(),
        ),
        out_specs=(P("chan", "tm", "height", None), P("chan", None, None)),
        check_vma=False,
    )
```

```python
import math

import jax
import jax.numpy as jnp
from jax import lax
from jax.sharding import PartitionSpec as P


def from_behind(block, axis, distance):
    devices = range(lax.axis_size(axis))
    route = [(i - distance, i) for i in devices if i - distance in devices]
    return lax.ppermute(block, axis, route)


def with_halo(array, sides, width):
    for axis, dim in sides:
        size, length = (lax.axis_size(axis), array.shape[dim])
        up = [(i, (i + 1) % size) for i in range(size - 1)]
        down = [(j, i) for i, j in up]
        last = lax.slice_in_dim(array, length - width, length, axis=dim)
        first = lax.slice_in_dim(array, 0, width, axis=dim)
        before = lax.ppermute(last, axis, up)
        after = lax.ppermute(first, axis, down)
        array = jnp.concatenate([before, array, after], axis=dim)
    return array


def gather_blocks(block, axis):
    size = lax.axis_size(axis)
    me = lax.axis_index(axis)
    got = [block] + [
        lax.ppermute(block, axis, [(j, (j + d) % size) for j in range(size)])
        for d in range(1, size)
    ]
    return jnp.concatenate(
        [lax.select_n((me - j) % size, *got) for j in range(size)], axis=0
    )


def on_device(features, cotangent, conv_weight, norm_gain, norm_bias):
    chans, frames, rows, cols = features.shape
    n_chan = lax.axis_size("chan")
    whole_x = gather_blocks(features, "chan")
    total = whole_x.shape[0]
    cells = frames * rows * cols
    flat_x = whole_x.reshape(total, cells).astype(jnp.float32)
    inv_rms = lax.rsqrt(jnp.mean(flat_x * flat_x, axis=0, keepdims=True) + 1e-06)
    normed = flat_x * inv_rms * norm_gain[:, None] + norm_bias[:, None]
    active = jax.nn.silu(normed).astype(jnp.bfloat16).reshape(total, frames, rows, cols)

    ahead = from_behind(lax.slice_in_dim(cotangent, 0, 2, axis=1), "tm", -1)
    longer = jnp.concatenate([cotangent, ahead], axis=1)
    bordered = with_halo(longer, (("height", 2),), 1)
    padded = jnp.pad(bordered, ((0, 0), (0, 0), (0, 0), (1, 1)))

    wdn = lax.ConvDimensionNumbers(
        lhs_spec=(1, 0, 2, 3, 4), rhs_spec=(1, 0, 2, 3, 4), out_spec=(0, 4, 1, 2, 3)
    )
    positions = frames * lax.axis_size("tm") * rows * lax.axis_size("height") * cols
    pieces = []
    half = chans // 2 if chans % 2 == 0 else chans
    for start in range(0, chans, half):
        flipped = lax.conv_general_dilated(
            padded[start : start + half][None],
            active[None],
            window_strides=(1, 1, 1),
            padding="VALID",
            dimension_numbers=wdn,
            preferred_element_type=jnp.float32,
        )
        summed = lax.psum(lax.rev(flipped, (1, 2, 3)), ("tm", "height"))
        pieces.append(summed / math.sqrt(positions))
    weight_grad = jnp.concatenate(pieces, axis=0).reshape(chans, 27, total)

    kernel = conv_weight.reshape(chans, 3, 3, 3, total)
    kernel = lax.rev(kernel, (1, 2, 3))
    adn = lax.ConvDimensionNumbers(
        lhs_spec=(0, 1, 2, 3, 4), rhs_spec=(4, 0, 1, 2, 3), out_spec=(0, 1, 2, 3, 4)
    )
    partial = lax.conv_general_dilated(
        padded[None],
        kernel,
        window_strides=(1, 1, 1),
        padding="VALID",
        dimension_numbers=adn,
        preferred_element_type=jnp.float32,
    )[0].reshape(total, cells)

    sig = jax.nn.sigmoid(normed)
    slope = sig * (1.0 + normed * (1.0 - sig)) * norm_gain[:, None]
    part_dots = jnp.sum(partial * slope * flat_x, axis=0, keepdims=True)
    packed = jnp.concatenate(
        [
            partial.reshape(n_chan, chans, cells),
            jnp.broadcast_to(part_dots[None], (n_chan, 1, cells)),
        ],
        axis=1,
    )
    mine = lax.psum_scatter(packed, "chan", scatter_dimension=0, tiled=True)[0]
    act_grad = mine[:chans]
    dots = mine[chans:]

    offset = lax.axis_index("chan") * chans
    own_x = features.reshape(chans, -1).astype(jnp.float32)
    own_slope = lax.dynamic_slice_in_dim(slope, offset, chans, 0)
    upstream = act_grad * own_slope
    own_back = inv_rms * upstream - own_x * inv_rms**3 * dots / total
    result = cotangent.reshape(chans, -1).astype(jnp.float32) + own_back
    return (result.astype(jnp.bfloat16).reshape(features.shape), weight_grad)


def solution(mesh):
    return jax.shard_map(
        on_device,
        mesh=mesh,
        in_specs=(
            P("chan", "tm", "height", None),
            P("chan", "tm", "height", None),
            P("chan", None, None),
            P(),
            P(),
        ),
        out_specs=(P("chan", "tm", "height", None), P("chan", None, None)),
        check_vma=False,
    )
```

```python
import math

import jax
import jax.numpy as jnp
from jax import lax
from jax.sharding import PartitionSpec as P


def from_behind(block, axis, distance):
    devices = range(lax.axis_size(axis))
    route = [(i - distance, i) for i in devices if i - distance in devices]
    return lax.ppermute(block, axis, route)


def with_halo(array, sides, width):
    for axis, dim in sides:
        size, length = (lax.axis_size(axis), array.shape[dim])
        up = [(i, (i + 1) % size) for i in range(size - 1)]
        down = [(j, i) for i, j in up]
        last = lax.slice_in_dim(array, length - width, length, axis=dim)
        first = lax.slice_in_dim(array, 0, width, axis=dim)
        before = lax.ppermute(last, axis, up)
        after = lax.ppermute(first, axis, down)
        array = jnp.concatenate([before, array, after], axis=dim)
    return array


def gather_blocks(block, axis):
    size = lax.axis_size(axis)
    me = lax.axis_index(axis)
    got = [block] + [
        lax.ppermute(block, axis, [(j, (j + d) % size) for j in range(size)])
        for d in range(1, size)
    ]
    return jnp.concatenate(
        [lax.select_n((me - j) % size, *got) for j in range(size)], axis=0
    )


def on_device(features, cotangent, conv_weight, norm_gain, norm_bias):
    chans, frames, rows, cols = features.shape
    n_chan = lax.axis_size("chan")
    whole_x = gather_blocks(features, "chan")
    total = whole_x.shape[0]
    cells = frames * rows * cols
    flat_x = whole_x.reshape(total, cells).astype(jnp.float32)
    inv_rms = lax.rsqrt(jnp.mean(flat_x * flat_x, axis=0, keepdims=True) + 1e-06)
    normed = flat_x * inv_rms * norm_gain[:, None] + norm_bias[:, None]
    active = jax.nn.silu(normed).astype(jnp.bfloat16).reshape(total, frames, rows, cols)

    ahead = from_behind(lax.slice_in_dim(cotangent, 0, 2, axis=1), "tm", -1)
    longer = jnp.concatenate([cotangent, ahead], axis=1)
    bordered = with_halo(longer, (("height", 2),), 1)
    padded = jnp.pad(bordered, ((0, 0), (0, 0), (0, 0), (1, 1)))

    positions = frames * lax.axis_size("tm") * rows * lax.axis_size("height") * cols
    cells_major = jnp.transpose(padded, (1, 2, 3, 0))
    taps = []
    for kt in range(3):
        for kh in range(3):
            for kw in range(3):
                taps.append(
                    cells_major[
                        2 - kt : 2 - kt + frames, 2 - kh : 2 - kh + rows, 2 - kw : 2 - kw + cols
                    ].reshape(cells, chans)
                )
    stacked = jnp.stack(taps, axis=0)
    active_t = jnp.transpose(active.reshape(total, cells))
    local_sums = lax.dot_general(
        stacked, active_t, (((1,), (0,)), ((), ())), preferred_element_type=jnp.float32
    )
    summed = lax.psum(local_sums, ("tm", "height"))
    weight_grad = jnp.transpose(summed / math.sqrt(positions), (1, 0, 2))

    kernel = conv_weight.reshape(chans, 3, 3, 3, total)
    kernel = lax.rev(kernel, (1, 2, 3))
    adn = lax.ConvDimensionNumbers(
        lhs_spec=(0, 1, 2, 3, 4), rhs_spec=(4, 0, 1, 2, 3), out_spec=(0, 1, 2, 3, 4)
    )
    partial = lax.conv_general_dilated(
        padded[None],
        kernel,
        window_strides=(1, 1, 1),
        padding="VALID",
        dimension_numbers=adn,
        preferred_element_type=jnp.float32,
    )[0].reshape(total, cells)

    sig = jax.nn.sigmoid(normed)
    slope = sig * (1.0 + normed * (1.0 - sig)) * norm_gain[:, None]
    part_dots = jnp.sum(partial * slope * flat_x, axis=0, keepdims=True)
    packed = jnp.concatenate(
        [
            partial.reshape(n_chan, chans, cells),
            jnp.broadcast_to(part_dots[None], (n_chan, 1, cells)),
        ],
        axis=1,
    )
    mine = lax.psum_scatter(packed, "chan", scatter_dimension=0, tiled=True)[0]
    act_grad = mine[:chans]
    dots = mine[chans:]

    offset = lax.axis_index("chan") * chans
    own_x = features.reshape(chans, -1).astype(jnp.float32)
    own_slope = lax.dynamic_slice_in_dim(slope, offset, chans, 0)
    upstream = act_grad * own_slope
    own_back = inv_rms * upstream - own_x * inv_rms**3 * dots / total
    result = cotangent.reshape(chans, -1).astype(jnp.float32) + own_back
    return (result.astype(jnp.bfloat16).reshape(features.shape), weight_grad)


def solution(mesh):
    return jax.shard_map(
        on_device,
        mesh=mesh,
        in_specs=(
            P("chan", "tm", "height", None),
            P("chan", "tm", "height", None),
            P("chan", None, None),
            P(),
            P(),
        ),
        out_specs=(P("chan", "tm", "height", None), P("chan", None, None)),
        check_vma=False,
    )
```

```python
import math

import jax
import jax.numpy as jnp
from jax import lax
from jax.experimental import pallas as pl
from jax.experimental.pallas import tpu as pltpu
from jax.sharding import PartitionSpec as P


def from_behind(block, axis, distance):
    devices = range(lax.axis_size(axis))
    route = [(i - distance, i) for i in devices if i - distance in devices]
    return lax.ppermute(block, axis, route)


def with_halo(array, sides, width):
    for axis, dim in sides:
        size, length = (lax.axis_size(axis), array.shape[dim])
        up = [(i, (i + 1) % size) for i in range(size - 1)]
        down = [(j, i) for i, j in up]
        last = lax.slice_in_dim(array, length - width, length, axis=dim)
        first = lax.slice_in_dim(array, 0, width, axis=dim)
        before = lax.ppermute(last, axis, up)
        after = lax.ppermute(first, axis, down)
        array = jnp.concatenate([before, array, after], axis=dim)
    return array


def gather_blocks(block, axis):
    size = lax.axis_size(axis)
    me = lax.axis_index(axis)
    got = [block] + [
        lax.ppermute(block, axis, [(j, (j + d) % size) for j in range(size)])
        for d in range(1, size)
    ]
    return jnp.concatenate(
        [lax.select_n((me - j) % size, *got) for j in range(size)], axis=0
    )


def weight_taps(shifted, active_t, frames, rows):
    _, _, _, cols, outs = shifted.shape
    cells, ins = active_t.shape

    def body(cot_ref, act_ref, out_ref):
        act = act_ref[...]
        for kt in range(3):
            for kh in range(3):
                for kw in range(3):
                    piece = cot_ref[kw, 2 - kt : 2 - kt + frames, 2 - kh : 2 - kh + rows]
                    out_ref[9 * kt + 3 * kh + kw] = lax.dot_general(
                        piece.reshape(cells, outs),
                        act,
                        (((0,), (0,)), ((), ())),
                        preferred_element_type=jnp.float32,
                    )

    return pl.pallas_call(
        body,
        out_shape=jax.ShapeDtypeStruct((27, outs, ins), jnp.float32),
        in_specs=[pl.BlockSpec(memory_space=pltpu.VMEM)] * 2,
        out_specs=pl.BlockSpec(memory_space=pltpu.VMEM),
        cost_estimate=pl.CostEstimate(
            flops=2 * 27 * ins * cells * outs,
            bytes_accessed=shifted.size * 2 + active_t.size * 2 + 27 * ins * outs * 4,
            transcendentals=0,
        ),
    )(shifted, active_t)


def halving_steps(axes):
    steps = []
    for axis in axes:
        size = lax.axis_size(axis)
        idx = lax.axis_index(axis)
        level = 1
        while level < size:
            steps.append((axis, level, (idx // level) % 2))
            level *= 2
    return steps


def exchange(block, axis, level):
    size = lax.axis_size(axis)
    return lax.ppermute(block, axis, [(i, i ^ level) for i in range(size)])


def halving_sum(x, steps):
    for axis, level, bit in steps:
        m = x.shape[0] // 2
        keep = lax.dynamic_slice_in_dim(x, bit * m, m, 0)
        send = lax.dynamic_slice_in_dim(x, (1 - bit) * m, m, 0)
        x = keep + exchange(send, axis, level)
    for axis, level, bit in reversed(steps):
        got = exchange(x, axis, level)
        m = x.shape[0]
        full = jnp.zeros((2 * m,) + x.shape[1:], x.dtype)
        full = lax.dynamic_update_slice_in_dim(full, x, bit * m, 0)
        x = lax.dynamic_update_slice_in_dim(full, got, (1 - bit) * m, 0)
    return x


def group_sum(x, near, far):
    near_steps, far_steps = halving_steps(near), halving_steps(far)
    unit = 2 ** (len(near_steps) + len(far_steps) + 1)
    rows = x.shape[0]
    padded_rows = -(-rows // unit) * unit
    x = jnp.pad(x, ((0, padded_rows - rows), (0, 0)))
    half = padded_rows // 2
    first = halving_sum(x[:half], near_steps + far_steps)
    second = halving_sum(x[half:], near_steps + far_steps[::-1])
    return jnp.concatenate([first, second], axis=0)[:rows]


def on_device(features, cotangent, conv_weight, norm_gain, norm_bias):
    chans, frames, rows, cols = features.shape
    n_chan = lax.axis_size("chan")
    whole_x = gather_blocks(features, "chan")
    total = whole_x.shape[0]
    cells = frames * rows * cols
    flat_x = whole_x.reshape(total, cells).astype(jnp.float32)
    inv_rms = lax.rsqrt(jnp.mean(flat_x * flat_x, axis=0, keepdims=True) + 1e-06)
    normed = flat_x * inv_rms * norm_gain[:, None] + norm_bias[:, None]
    active = jax.nn.silu(normed).astype(jnp.bfloat16).reshape(total, frames, rows, cols)

    ahead = from_behind(lax.slice_in_dim(cotangent, 0, 2, axis=1), "tm", -1)
    longer = jnp.concatenate([cotangent, ahead], axis=1)
    bordered = with_halo(longer, (("height", 2),), 1)
    padded = jnp.pad(bordered, ((0, 0), (0, 0), (0, 0), (1, 1)))

    positions = frames * lax.axis_size("tm") * rows * lax.axis_size("height") * cols
    cells_major = jnp.transpose(padded, (1, 2, 3, 0))
    shifted = jnp.stack(
        [cells_major[:, :, 2 - kw : 2 - kw + cols] for kw in range(3)], axis=0
    )
    active_t = jnp.transpose(active.reshape(total, cells))
    local_sums = weight_taps(shifted, active_t, frames, rows)
    summed = group_sum(local_sums.reshape(27 * chans, total), ("height",), ("tm",))
    weight_grad = jnp.transpose(
        (summed / math.sqrt(positions)).reshape(27, chans, total), (1, 0, 2)
    )

    kernel = conv_weight.reshape(chans, 3, 3, 3, total)
    kernel = lax.rev(kernel, (1, 2, 3))
    adn = lax.ConvDimensionNumbers(
        lhs_spec=(0, 1, 2, 3, 4), rhs_spec=(4, 0, 1, 2, 3), out_spec=(0, 1, 2, 3, 4)
    )
    partial = lax.conv_general_dilated(
        padded[None],
        kernel,
        window_strides=(1, 1, 1),
        padding="VALID",
        dimension_numbers=adn,
        preferred_element_type=jnp.float32,
    )[0].reshape(total, cells)

    sig = jax.nn.sigmoid(normed)
    slope = sig * (1.0 + normed * (1.0 - sig)) * norm_gain[:, None]
    part_dots = jnp.sum(partial * slope * flat_x, axis=0, keepdims=True)
    packed = jnp.concatenate(
        [
            partial.reshape(n_chan, chans, cells),
            jnp.broadcast_to(part_dots[None], (n_chan, 1, cells)),
        ],
        axis=1,
    )
    mine = lax.psum_scatter(packed, "chan", scatter_dimension=0, tiled=True)[0]
    act_grad = mine[:chans]
    dots = mine[chans:]

    offset = lax.axis_index("chan") * chans
    own_x = features.reshape(chans, -1).astype(jnp.float32)
    own_slope = lax.dynamic_slice_in_dim(slope, offset, chans, 0)
    upstream = act_grad * own_slope
    own_back = inv_rms * upstream - own_x * inv_rms**3 * dots / total
    result = cotangent.reshape(chans, -1).astype(jnp.float32) + own_back
    return (result.astype(jnp.bfloat16).reshape(features.shape), weight_grad)


def solution(mesh):
    return jax.shard_map(
        on_device,
        mesh=mesh,
        in_specs=(
            P("chan", "tm", "height", None),
            P("chan", "tm", "height", None),
            P("chan", None, None),
            P(),
            P(),
        ),
        out_specs=(P("chan", "tm", "height", None), P("chan", None, None)),
        check_vma=False,
    )
```

```python
import math

import jax
import jax.numpy as jnp
from jax import lax
from jax.experimental import pallas as pl
from jax.experimental.pallas import tpu as pltpu
from jax.sharding import PartitionSpec as P


def from_behind(block, axis, distance):
    devices = range(lax.axis_size(axis))
    route = [(i - distance, i) for i in devices if i - distance in devices]
    return lax.ppermute(block, axis, route)


def with_halo(array, sides, width):
    for axis, dim in sides:
        size, length = (lax.axis_size(axis), array.shape[dim])
        up = [(i, (i + 1) % size) for i in range(size - 1)]
        down = [(j, i) for i, j in up]
        last = lax.slice_in_dim(array, length - width, length, axis=dim)
        first = lax.slice_in_dim(array, 0, width, axis=dim)
        before = lax.ppermute(last, axis, up)
        after = lax.ppermute(first, axis, down)
        array = jnp.concatenate([before, array, after], axis=dim)
    return array


def gather_blocks(block, axis):
    size = lax.axis_size(axis)
    me = lax.axis_index(axis)
    got = [block] + [
        lax.ppermute(block, axis, [(j, (j + d) % size) for j in range(size)])
        for d in range(1, size)
    ]
    return jnp.concatenate(
        [lax.select_n((me - j) % size, *got) for j in range(size)], axis=0
    )


def weight_taps(shifted, active_t, frames, rows):
    _, _, _, cols, outs = shifted.shape
    cells, ins = active_t.shape

    def body(cot_ref, act_ref, out_ref):
        act = act_ref[...]
        for kt in range(3):
            for kh in range(3):
                for kw in range(3):
                    piece = cot_ref[kw, 2 - kt : 2 - kt + frames, 2 - kh : 2 - kh + rows]
                    out_ref[9 * kt + 3 * kh + kw] = lax.dot_general(
                        piece.reshape(cells, outs),
                        act,
                        (((0,), (0,)), ((), ())),
                        preferred_element_type=jnp.float32,
                    )

    return pl.pallas_call(
        body,
        out_shape=jax.ShapeDtypeStruct((27, outs, ins), jnp.float32),
        in_specs=[pl.BlockSpec(memory_space=pltpu.VMEM)] * 2,
        out_specs=pl.BlockSpec(memory_space=pltpu.VMEM),
        cost_estimate=pl.CostEstimate(
            flops=2 * 27 * ins * cells * outs,
            bytes_accessed=shifted.size * 2 + active_t.size * 2 + 27 * ins * outs * 4,
            transcendentals=0,
        ),
    )(shifted, active_t)


def halving_steps(axes):
    steps = []
    for axis in axes:
        size = lax.axis_size(axis)
        idx = lax.axis_index(axis)
        level = 1
        while level < size:
            steps.append((axis, level, (idx // level) % 2))
            level *= 2
    return steps


def exchange(block, axis, level):
    size = lax.axis_size(axis)
    return lax.ppermute(block, axis, [(i, i ^ level) for i in range(size)])


def halving_sum(x, steps):
    for axis, level, bit in steps:
        m = x.shape[0] // 2
        keep = lax.dynamic_slice_in_dim(x, bit * m, m, 0)
        send = lax.dynamic_slice_in_dim(x, (1 - bit) * m, m, 0)
        x = keep + exchange(send, axis, level)
    for axis, level, bit in reversed(steps):
        got = exchange(x, axis, level)
        x = lax.select_n(
            bit, jnp.concatenate([x, got], axis=0), jnp.concatenate([got, x], axis=0)
        )
    return x


def group_sum(x, near, far):
    near_steps, far_steps = halving_steps(near), halving_steps(far)
    unit = 2 ** (len(near_steps) + len(far_steps) + 1)
    rows = x.shape[0]
    padded_rows = -(-rows // unit) * unit
    x = jnp.pad(x, ((0, padded_rows - rows), (0, 0)))
    half = padded_rows // 2
    first = halving_sum(x[:half], near_steps + far_steps)
    second = halving_sum(x[half:], near_steps + far_steps[::-1])
    return jnp.concatenate([first, second], axis=0)[:rows]


def on_device(features, cotangent, conv_weight, norm_gain, norm_bias):
    chans, frames, rows, cols = features.shape
    n_chan = lax.axis_size("chan")
    whole_x = gather_blocks(features, "chan")
    total = whole_x.shape[0]
    cells = frames * rows * cols
    flat_x = whole_x.reshape(total, cells).astype(jnp.float32)
    inv_rms = lax.rsqrt(jnp.mean(flat_x * flat_x, axis=0, keepdims=True) + 1e-06)
    normed = flat_x * inv_rms * norm_gain[:, None] + norm_bias[:, None]
    active = jax.nn.silu(normed).astype(jnp.bfloat16).reshape(total, frames, rows, cols)

    ahead = from_behind(lax.slice_in_dim(cotangent, 0, 2, axis=1), "tm", -1)
    longer = jnp.concatenate([cotangent, ahead], axis=1)
    bordered = with_halo(longer, (("height", 2),), 1)
    padded = jnp.pad(bordered, ((0, 0), (0, 0), (0, 0), (1, 1)))

    kernel = conv_weight.reshape(chans, 3, 3, 3, total)
    kernel = lax.rev(kernel, (1, 2, 3))
    adn = lax.ConvDimensionNumbers(
        lhs_spec=(0, 1, 2, 3, 4), rhs_spec=(4, 0, 1, 2, 3), out_spec=(0, 1, 2, 3, 4)
    )
    partial = lax.conv_general_dilated(
        padded[None],
        kernel,
        window_strides=(1, 1, 1),
        padding="VALID",
        dimension_numbers=adn,
        preferred_element_type=jnp.float32,
    )[0].reshape(total, cells)

    sig = jax.nn.sigmoid(normed)
    slope = sig * (1.0 + normed * (1.0 - sig)) * norm_gain[:, None]
    part_dots = jnp.sum(partial * slope * flat_x, axis=0, keepdims=True)
    packed = jnp.concatenate(
        [
            partial.reshape(n_chan, chans, cells),
            jnp.broadcast_to(part_dots[None], (n_chan, 1, cells)),
        ],
        axis=1,
    )
    packed, padded, active = lax.optimization_barrier((packed, padded, active))
    positions = frames * lax.axis_size("tm") * rows * lax.axis_size("height") * cols
    cells_major = jnp.transpose(padded, (1, 2, 3, 0))
    shifted = jnp.stack(
        [cells_major[:, :, 2 - kw : 2 - kw + cols] for kw in range(3)], axis=0
    )
    active_t = jnp.transpose(active.reshape(total, cells))
    local_sums = weight_taps(shifted, active_t, frames, rows)
    summed = group_sum(local_sums.reshape(27 * chans, total), ("height",), ("tm",))
    weight_grad = jnp.transpose(
        (summed / math.sqrt(positions)).reshape(27, chans, total), (1, 0, 2)
    )

    mine = lax.psum_scatter(packed, "chan", scatter_dimension=0, tiled=True)[0]
    act_grad = mine[:chans]
    dots = mine[chans:]

    offset = lax.axis_index("chan") * chans
    own_x = features.reshape(chans, -1).astype(jnp.float32)
    own_slope = lax.dynamic_slice_in_dim(slope, offset, chans, 0)
    upstream = act_grad * own_slope
    own_back = inv_rms * upstream - own_x * inv_rms**3 * dots / total
    result = cotangent.reshape(chans, -1).astype(jnp.float32) + own_back
    return (result.astype(jnp.bfloat16).reshape(features.shape), weight_grad)


def solution(mesh):
    return jax.shard_map(
        on_device,
        mesh=mesh,
        in_specs=(
            P("chan", "tm", "height", None),
            P("chan", "tm", "height", None),
            P("chan", None, None),
            P(),
            P(),
        ),
        out_specs=(P("chan", "tm", "height", None), P("chan", None, None)),
        check_vma=False,
    )
```

```python
import math

import jax
import jax.numpy as jnp
from jax import lax
from jax.experimental import pallas as pl
from jax.experimental.pallas import tpu as pltpu
from jax.sharding import PartitionSpec as P


def from_behind(block, axis, distance):
    devices = range(lax.axis_size(axis))
    route = [(i - distance, i) for i in devices if i - distance in devices]
    return lax.ppermute(block, axis, route)


def with_halo(array, sides, width):
    for axis, dim in sides:
        size, length = (lax.axis_size(axis), array.shape[dim])
        up = [(i, (i + 1) % size) for i in range(size - 1)]
        down = [(j, i) for i, j in up]
        last = lax.slice_in_dim(array, length - width, length, axis=dim)
        first = lax.slice_in_dim(array, 0, width, axis=dim)
        before = lax.ppermute(last, axis, up)
        after = lax.ppermute(first, axis, down)
        array = jnp.concatenate([before, array, after], axis=dim)
    return array


def gather_blocks(block, axis):
    size = lax.axis_size(axis)
    me = lax.axis_index(axis)
    got = [block] + [
        lax.ppermute(block, axis, [(j, (j + d) % size) for j in range(size)])
        for d in range(1, size)
    ]
    return jnp.concatenate(
        [lax.select_n((me - j) % size, *got) for j in range(size)], axis=0
    )


def weight_taps(shifted, active_t, anchor, frames, rows):
    _, _, _, cols, outs = shifted.shape
    cells, ins = active_t.shape

    def body(cot_ref, act_ref, anchor_ref, out_ref):
        act = act_ref[...]
        for kt in range(3):
            for kh in range(3):
                for kw in range(3):
                    piece = cot_ref[kw, 2 - kt : 2 - kt + frames, 2 - kh : 2 - kh + rows]
                    out_ref[9 * kt + 3 * kh + kw] = lax.dot_general(
                        piece.reshape(cells, outs),
                        act,
                        (((0,), (0,)), ((), ())),
                        preferred_element_type=jnp.float32,
                    )

    return pl.pallas_call(
        body,
        out_shape=jax.ShapeDtypeStruct((27, outs, ins), jnp.float32),
        in_specs=[pl.BlockSpec(memory_space=pltpu.VMEM)] * 3,
        out_specs=pl.BlockSpec(memory_space=pltpu.VMEM),
        cost_estimate=pl.CostEstimate(
            flops=2 * 27 * ins * cells * outs,
            bytes_accessed=shifted.size * 2 + active_t.size * 2 + 27 * ins * outs * 4,
            transcendentals=0,
        ),
    )(shifted, active_t, anchor)


def halving_steps(axes):
    steps = []
    for axis in axes:
        size = lax.axis_size(axis)
        idx = lax.axis_index(axis)
        level = 1
        while level < size:
            steps.append((axis, level, (idx // level) % 2))
            level *= 2
    return steps


def exchange(block, axis, level):
    size = lax.axis_size(axis)
    return lax.ppermute(block, axis, [(i, i ^ level) for i in range(size)])


def halving_sum(x, steps):
    for axis, level, bit in steps:
        m = x.shape[0] // 2
        keep = lax.dynamic_slice_in_dim(x, bit * m, m, 0)
        send = lax.dynamic_slice_in_dim(x, (1 - bit) * m, m, 0)
        x = keep + exchange(send, axis, level)
    for axis, level, bit in reversed(steps):
        got = exchange(x, axis, level)
        x = lax.select_n(
            bit, jnp.concatenate([x, got], axis=0), jnp.concatenate([got, x], axis=0)
        )
    return x


def xor_sum(x, axis):
    size = lax.axis_size(axis)
    level = 1
    while level < size:
        x = x + exchange(x, axis, level)
        level *= 2
    return x


def group_sum(x, near, far):
    near_steps, far_steps = halving_steps(near), halving_steps(far)
    unit = 2 ** (len(near_steps) + len(far_steps) + 1)
    rows = x.shape[0]
    padded_rows = -(-rows // unit) * unit
    x = jnp.pad(x, ((0, padded_rows - rows), (0, 0)))
    half = padded_rows // 2
    first = halving_sum(x[:half], near_steps + far_steps)
    second = halving_sum(x[half:], near_steps + far_steps[::-1])
    return jnp.concatenate([first, second], axis=0)[:rows]


def on_device(features, cotangent, conv_weight, norm_gain, norm_bias):
    chans, frames, rows, cols = features.shape
    n_chan = lax.axis_size("chan")
    whole_x = gather_blocks(features, "chan")
    total = whole_x.shape[0]
    cells = frames * rows * cols
    flat_x = whole_x.reshape(total, cells).astype(jnp.float32)
    inv_rms = lax.rsqrt(jnp.mean(flat_x * flat_x, axis=0, keepdims=True) + 1e-06)
    normed = flat_x * inv_rms * norm_gain[:, None] + norm_bias[:, None]
    active = jax.nn.silu(normed).astype(jnp.bfloat16).reshape(total, frames, rows, cols)

    ahead = from_behind(lax.slice_in_dim(cotangent, 0, 2, axis=1), "tm", -1)
    longer = jnp.concatenate([cotangent, ahead], axis=1)
    bordered = with_halo(longer, (("height", 2),), 1)
    padded = jnp.pad(bordered, ((0, 0), (0, 0), (0, 0), (1, 1)))

    kernel = conv_weight.reshape(chans, 3, 3, 3, total)
    kernel = lax.rev(kernel, (1, 2, 3))
    adn = lax.ConvDimensionNumbers(
        lhs_spec=(0, 1, 2, 3, 4), rhs_spec=(4, 0, 1, 2, 3), out_spec=(0, 1, 2, 3, 4)
    )
    partial = lax.conv_general_dilated(
        padded[None],
        kernel,
        window_strides=(1, 1, 1),
        padding="VALID",
        dimension_numbers=adn,
        preferred_element_type=jnp.float32,
    )[0].reshape(total, cells)

    mine = lax.psum_scatter(
        partial.reshape(n_chan, chans, cells), "chan", scatter_dimension=0, tiled=True
    )[0]

    positions = frames * lax.axis_size("tm") * rows * lax.axis_size("height") * cols
    cells_major = jnp.transpose(padded, (1, 2, 3, 0))
    shifted = jnp.stack(
        [cells_major[:, :, 2 - kw : 2 - kw + cols] for kw in range(3)], axis=0
    )
    active_t = jnp.transpose(active.reshape(total, cells))
    local_sums = weight_taps(shifted, active_t, partial[:8, :128], frames, rows)
    summed = group_sum(local_sums.reshape(27 * chans, total), ("height",), ("tm",))
    weight_grad = jnp.transpose(
        (summed / math.sqrt(positions)).reshape(27, chans, total), (1, 0, 2)
    )

    offset = lax.axis_index("chan") * chans
    own_x = features.reshape(chans, -1).astype(jnp.float32)
    own_normed = lax.dynamic_slice_in_dim(normed, offset, chans, 0)
    own_gain = lax.dynamic_slice_in_dim(norm_gain, offset, chans, 0)
    sig = jax.nn.sigmoid(own_normed)
    upstream = mine * (sig * (1.0 + own_normed * (1.0 - sig))) * own_gain[:, None]
    dots = xor_sum(jnp.sum(upstream * own_x, axis=0, keepdims=True), "chan")
    own_back = inv_rms * upstream - own_x * inv_rms**3 * dots / total
    result = cotangent.reshape(chans, -1).astype(jnp.float32) + own_back
    return (result.astype(jnp.bfloat16).reshape(features.shape), weight_grad)


def solution(mesh):
    return jax.shard_map(
        on_device,
        mesh=mesh,
        in_specs=(
            P("chan", "tm", "height", None),
            P("chan", "tm", "height", None),
            P("chan", None, None),
            P(),
            P(),
        ),
        out_specs=(P("chan", "tm", "height", None), P("chan", None, None)),
        check_vma=False,
    )
```

```python
import math

import jax
import jax.numpy as jnp
from jax import lax
from jax.experimental import pallas as pl
from jax.experimental.pallas import tpu as pltpu
from jax.sharding import PartitionSpec as P


def from_behind(block, axis, distance):
    devices = range(lax.axis_size(axis))
    route = [(i - distance, i) for i in devices if i - distance in devices]
    return lax.ppermute(block, axis, route)


def with_halo(array, sides, width):
    for axis, dim in sides:
        size, length = (lax.axis_size(axis), array.shape[dim])
        up = [(i, (i + 1) % size) for i in range(size - 1)]
        down = [(j, i) for i, j in up]
        last = lax.slice_in_dim(array, length - width, length, axis=dim)
        first = lax.slice_in_dim(array, 0, width, axis=dim)
        before = lax.ppermute(last, axis, up)
        after = lax.ppermute(first, axis, down)
        array = jnp.concatenate([before, array, after], axis=dim)
    return array


def gather_blocks(block, axis):
    size = lax.axis_size(axis)
    me = lax.axis_index(axis)
    got = [block] + [
        lax.ppermute(block, axis, [(j, (j + d) % size) for j in range(size)])
        for d in range(1, size)
    ]
    return jnp.concatenate(
        [lax.select_n((me - j) % size, *got) for j in range(size)], axis=0
    )


def weight_taps(shifted, active_t, frames, rows):
    _, _, _, cols, outs = shifted.shape
    cells, ins = active_t.shape

    def body(cot_ref, act_ref, out_ref):
        act = act_ref[...]
        for kt in range(3):
            for kh in range(3):
                for kw in range(3):
                    piece = cot_ref[kw, 2 - kt : 2 - kt + frames, 2 - kh : 2 - kh + rows]
                    out_ref[9 * kt + 3 * kh + kw] = lax.dot_general(
                        piece.reshape(cells, outs),
                        act,
                        (((0,), (0,)), ((), ())),
                        preferred_element_type=jnp.float32,
                    )

    return pl.pallas_call(
        body,
        out_shape=jax.ShapeDtypeStruct((27, outs, ins), jnp.float32),
        in_specs=[pl.BlockSpec(memory_space=pltpu.VMEM)] * 2,
        out_specs=pl.BlockSpec(memory_space=pltpu.VMEM),
        cost_estimate=pl.CostEstimate(
            flops=2 * 27 * ins * cells * outs,
            bytes_accessed=shifted.size * 2 + active_t.size * 2 + 27 * ins * outs * 4,
            transcendentals=0,
        ),
    )(shifted, active_t)


def halving_steps(axes):
    steps = []
    for axis in axes:
        size = lax.axis_size(axis)
        idx = lax.axis_index(axis)
        level = 1
        while level < size:
            steps.append((axis, level, (idx // level) % 2))
            level *= 2
    return steps


def exchange(block, axis, level):
    size = lax.axis_size(axis)
    return lax.ppermute(block, axis, [(i, i ^ level) for i in range(size)])


def halving_sum(x, steps):
    for axis, level, bit in steps:
        m = x.shape[0] // 2
        keep = lax.dynamic_slice_in_dim(x, bit * m, m, 0)
        send = lax.dynamic_slice_in_dim(x, (1 - bit) * m, m, 0)
        x = keep + exchange(send, axis, level)
    for axis, level, bit in reversed(steps):
        got = exchange(x, axis, level)
        x = lax.select_n(
            bit, jnp.concatenate([x, got], axis=0), jnp.concatenate([got, x], axis=0)
        )
    return x


def group_sum(x, near, far):
    near_steps, far_steps = halving_steps(near), halving_steps(far)
    unit = 2 ** (len(near_steps) + len(far_steps) + 1)
    rows = x.shape[0]
    padded_rows = -(-rows // unit) * unit
    x = jnp.pad(x, ((0, padded_rows - rows), (0, 0)))
    half = padded_rows // 2
    first = halving_sum(x[:half], near_steps + far_steps)
    second = halving_sum(x[half:], near_steps + far_steps[::-1])
    return jnp.concatenate([first, second], axis=0)[:rows]


def on_device(features, cotangent, conv_weight, norm_gain, norm_bias):
    chans, frames, rows, cols = features.shape
    n_chan = lax.axis_size("chan")
    whole_x = gather_blocks(features, "chan")
    total = whole_x.shape[0]
    cells = frames * rows * cols
    flat_x = whole_x.reshape(total, cells).astype(jnp.float32)
    inv_rms = lax.rsqrt(jnp.mean(flat_x * flat_x, axis=0, keepdims=True) + 1e-06)
    normed = flat_x * inv_rms * norm_gain[:, None] + norm_bias[:, None]
    active = jax.nn.silu(normed).astype(jnp.bfloat16).reshape(total, frames, rows, cols)

    ahead = from_behind(lax.slice_in_dim(cotangent, 0, 2, axis=1), "tm", -1)
    longer = jnp.concatenate([cotangent, ahead], axis=1)
    bordered = with_halo(longer, (("height", 2),), 1)
    padded = jnp.pad(bordered, ((0, 0), (0, 0), (0, 0), (1, 1)))

    positions = frames * lax.axis_size("tm") * rows * lax.axis_size("height") * cols
    cells_major = jnp.transpose(padded, (1, 2, 3, 0))
    shifted = jnp.stack(
        [cells_major[:, :, 2 - kw : 2 - kw + cols] for kw in range(3)], axis=0
    )
    active_t = jnp.transpose(active.reshape(total, cells))
    local_sums = weight_taps(shifted, active_t, frames, rows)
    summed = group_sum(local_sums.reshape(27 * chans, total), ("height",), ("tm",))
    weight_grad = jnp.transpose(
        (summed / math.sqrt(positions)).reshape(27, chans, total), (1, 0, 2)
    )

    kernel = conv_weight.reshape(chans, 3, 3, 3, total)
    kernel = lax.rev(kernel, (1, 2, 3))
    adn = lax.ConvDimensionNumbers(
        lhs_spec=(0, 1, 2, 3, 4), rhs_spec=(4, 0, 1, 2, 3), out_spec=(0, 1, 2, 3, 4)
    )
    partial = lax.conv_general_dilated(
        padded[None],
        kernel,
        window_strides=(1, 1, 1),
        padding="VALID",
        dimension_numbers=adn,
        preferred_element_type=jnp.float32,
    )[0].reshape(total, cells)

    sig = jax.nn.sigmoid(normed)
    slope = sig * (1.0 + normed * (1.0 - sig)) * norm_gain[:, None]
    part_dots = jnp.sum(partial * slope * flat_x, axis=0, keepdims=True)
    packed = jnp.concatenate(
        [
            partial.reshape(n_chan, chans, cells),
            jnp.broadcast_to(part_dots[None], (n_chan, 1, cells)),
        ],
        axis=1,
    )
    mine = lax.psum_scatter(packed, "chan", scatter_dimension=0, tiled=True)[0]
    act_grad = mine[:chans]
    dots = mine[chans:]

    offset = lax.axis_index("chan") * chans
    own_x = features.reshape(chans, -1).astype(jnp.float32)
    own_slope = lax.dynamic_slice_in_dim(slope, offset, chans, 0)
    upstream = act_grad * own_slope
    own_back = inv_rms * upstream - own_x * inv_rms**3 * dots / total
    result = cotangent.reshape(chans, -1).astype(jnp.float32) + own_back
    return (result.astype(jnp.bfloat16).reshape(features.shape), weight_grad)


def solution(mesh):
    return jax.shard_map(
        on_device,
        mesh=mesh,
        in_specs=(
            P("chan", "tm", "height", None),
            P("chan", "tm", "height", None),
            P("chan", None, None),
            P(),
            P(),
        ),
        out_specs=(P("chan", "tm", "height", None), P("chan", None, None)),
        check_vma=False,
    )
```

```python
import math

import jax
import jax.numpy as jnp
from jax import lax
from jax.experimental import pallas as pl
from jax.experimental.pallas import tpu as pltpu
from jax.sharding import PartitionSpec as P


def from_behind(block, axis, distance):
    devices = range(lax.axis_size(axis))
    route = [(i - distance, i) for i in devices if i - distance in devices]
    return lax.ppermute(block, axis, route)


def with_halo(array, sides, width):
    for axis, dim in sides:
        size, length = (lax.axis_size(axis), array.shape[dim])
        up = [(i, (i + 1) % size) for i in range(size - 1)]
        down = [(j, i) for i, j in up]
        last = lax.slice_in_dim(array, length - width, length, axis=dim)
        first = lax.slice_in_dim(array, 0, width, axis=dim)
        before = lax.ppermute(last, axis, up)
        after = lax.ppermute(first, axis, down)
        array = jnp.concatenate([before, array, after], axis=dim)
    return array


def gather_blocks(block, axis):
    size = lax.axis_size(axis)
    me = lax.axis_index(axis)
    got = [block] + [
        lax.ppermute(block, axis, [(j, (j + d) % size) for j in range(size)])
        for d in range(1, size)
    ]
    return jnp.concatenate(
        [lax.select_n((me - j) % size, *got) for j in range(size)], axis=0
    )


def tap_kernel(shifted, active_t, weight_t, frames, rows):
    _, _, _, cols, outs = shifted.shape
    cells, ins = active_t.shape

    def body(cot_ref, act_ref, w_ref, wg_ref, ag_ref):
        act = act_ref[...]
        for kt in range(3):
            for kh in range(3):
                for kw in range(3):
                    k = 9 * kt + 3 * kh + kw
                    piece = cot_ref[kw, 2 - kt : 2 - kt + frames, 2 - kh : 2 - kh + rows]
                    piece = piece.reshape(cells, outs)
                    wg_ref[k] = lax.dot_general(
                        piece, act, (((0,), (0,)), ((), ())),
                        preferred_element_type=jnp.float32,
                    )
                    term = jnp.dot(piece, w_ref[k], preferred_element_type=jnp.float32)
                    if k == 0:
                        ag_ref[...] = term
                    else:
                        ag_ref[...] += term

    return pl.pallas_call(
        body,
        out_shape=(
            jax.ShapeDtypeStruct((27, outs, ins), jnp.float32),
            jax.ShapeDtypeStruct((cells, ins), jnp.float32),
        ),
        in_specs=[pl.BlockSpec(memory_space=pltpu.VMEM)] * 3,
        out_specs=(
            pl.BlockSpec(memory_space=pltpu.VMEM),
            pl.BlockSpec(memory_space=pltpu.VMEM),
        ),
        cost_estimate=pl.CostEstimate(
            flops=4 * 27 * ins * cells * outs,
            bytes_accessed=shifted.size * 2 + active_t.size * 2 + weight_t.size * 2
            + 27 * ins * outs * 4 + cells * ins * 4,
            transcendentals=0,
        ),
    )(shifted, active_t, weight_t)


def halving_steps(axes):
    steps = []
    for axis in axes:
        size = lax.axis_size(axis)
        idx = lax.axis_index(axis)
        level = 1
        while level < size:
            steps.append((axis, level, (idx // level) % 2))
            level *= 2
    return steps


def exchange(block, axis, level):
    size = lax.axis_size(axis)
    return lax.ppermute(block, axis, [(i, i ^ level) for i in range(size)])


def halving_sum(x, steps):
    for axis, level, bit in steps:
        m = x.shape[0] // 2
        keep = lax.dynamic_slice_in_dim(x, bit * m, m, 0)
        send = lax.dynamic_slice_in_dim(x, (1 - bit) * m, m, 0)
        x = keep + exchange(send, axis, level)
    for axis, level, bit in reversed(steps):
        got = exchange(x, axis, level)
        x = lax.select_n(
            bit, jnp.concatenate([x, got], axis=0), jnp.concatenate([got, x], axis=0)
        )
    return x


def group_sum(x, near, far):
    near_steps, far_steps = halving_steps(near), halving_steps(far)
    unit = 2 ** (len(near_steps) + len(far_steps) + 1)
    rows = x.shape[0]
    padded_rows = -(-rows // unit) * unit
    x = jnp.pad(x, ((0, padded_rows - rows), (0, 0)))
    half = padded_rows // 2
    first = halving_sum(x[:half], near_steps + far_steps)
    second = halving_sum(x[half:], near_steps + far_steps[::-1])
    return jnp.concatenate([first, second], axis=0)[:rows]


def on_device(features, cotangent, conv_weight, norm_gain, norm_bias):
    chans, frames, rows, cols = features.shape
    n_chan = lax.axis_size("chan")
    whole_x = gather_blocks(features, "chan")
    total = whole_x.shape[0]
    cells = frames * rows * cols
    flat_x = whole_x.reshape(total, cells).astype(jnp.float32)
    inv_rms = lax.rsqrt(jnp.mean(flat_x * flat_x, axis=0, keepdims=True) + 1e-06)
    normed = flat_x * inv_rms * norm_gain[:, None] + norm_bias[:, None]
    active = jax.nn.silu(normed).astype(jnp.bfloat16).reshape(total, frames, rows, cols)

    ahead = from_behind(lax.slice_in_dim(cotangent, 0, 2, axis=1), "tm", -1)
    longer = jnp.concatenate([cotangent, ahead], axis=1)
    bordered = with_halo(longer, (("height", 2),), 1)
    padded = jnp.pad(bordered, ((0, 0), (0, 0), (0, 0), (1, 1)))

    positions = frames * lax.axis_size("tm") * rows * lax.axis_size("height") * cols
    cells_major = jnp.transpose(padded, (1, 2, 3, 0))
    shifted = jnp.stack(
        [cells_major[:, :, 2 - kw : 2 - kw + cols] for kw in range(3)], axis=0
    )
    active_t = jnp.transpose(active.reshape(total, cells))
    weight_t = jnp.transpose(conv_weight, (1, 0, 2))
    local_sums, act_part = tap_kernel(shifted, active_t, weight_t, frames, rows)
    partial = jnp.transpose(act_part)
    summed = group_sum(local_sums.reshape(27 * chans, total), ("height",), ("tm",))
    weight_grad = jnp.transpose(
        (summed / math.sqrt(positions)).reshape(27, chans, total), (1, 0, 2)
    )

    sig = jax.nn.sigmoid(normed)
    slope = sig * (1.0 + normed * (1.0 - sig)) * norm_gain[:, None]
    part_dots = jnp.sum(partial * slope * flat_x, axis=0, keepdims=True)
    packed = jnp.concatenate(
        [
            partial.reshape(n_chan, chans, cells),
            jnp.broadcast_to(part_dots[None], (n_chan, 1, cells)),
        ],
        axis=1,
    )
    mine = lax.psum_scatter(packed, "chan", scatter_dimension=0, tiled=True)[0]
    act_grad = mine[:chans]
    dots = mine[chans:]

    offset = lax.axis_index("chan") * chans
    own_x = features.reshape(chans, -1).astype(jnp.float32)
    own_slope = lax.dynamic_slice_in_dim(slope, offset, chans, 0)
    upstream = act_grad * own_slope
    own_back = inv_rms * upstream - own_x * inv_rms**3 * dots / total
    result = cotangent.reshape(chans, -1).astype(jnp.float32) + own_back
    return (result.astype(jnp.bfloat16).reshape(features.shape), weight_grad)


def solution(mesh):
    return jax.shard_map(
        on_device,
        mesh=mesh,
        in_specs=(
            P("chan", "tm", "height", None),
            P("chan", "tm", "height", None),
            P("chan", None, None),
            P(),
            P(),
        ),
        out_specs=(P("chan", "tm", "height", None), P("chan", None, None)),
        check_vma=False,
    )
```

```python
import math

import jax
import jax.numpy as jnp
from jax import lax
from jax.experimental import pallas as pl
from jax.experimental.pallas import tpu as pltpu
from jax.sharding import PartitionSpec as P


def from_behind(block, axis, distance):
    devices = range(lax.axis_size(axis))
    route = [(i - distance, i) for i in devices if i - distance in devices]
    return lax.ppermute(block, axis, route)


def with_halo(array, sides, width):
    for axis, dim in sides:
        size, length = (lax.axis_size(axis), array.shape[dim])
        up = [(i, (i + 1) % size) for i in range(size - 1)]
        down = [(j, i) for i, j in up]
        last = lax.slice_in_dim(array, length - width, length, axis=dim)
        first = lax.slice_in_dim(array, 0, width, axis=dim)
        before = lax.ppermute(last, axis, up)
        after = lax.ppermute(first, axis, down)
        array = jnp.concatenate([before, array, after], axis=dim)
    return array


def gather_blocks(block, axis):
    size = lax.axis_size(axis)
    me = lax.axis_index(axis)
    got = [block] + [
        lax.ppermute(block, axis, [(j, (j + d) % size) for j in range(size)])
        for d in range(1, size)
    ]
    return jnp.concatenate(
        [lax.select_n((me - j) % size, *got) for j in range(size)], axis=0
    )


def tap_kernel(shifted, active_t, weight_t, slope_x, n_chan, frames, rows):
    _, _, _, cols, outs = shifted.shape
    cells, ins = active_t.shape
    block = ins // n_chan

    def body(cot_ref, act_ref, w_ref, sx_ref, wg_ref, pk_ref, ag_ref):
        act = act_ref[...]
        for kt in range(3):
            for kh in range(3):
                for kw in range(3):
                    k = 9 * kt + 3 * kh + kw
                    piece = cot_ref[kw, 2 - kt : 2 - kt + frames, 2 - kh : 2 - kh + rows]
                    piece = piece.reshape(cells, outs)
                    wg_ref[k] = lax.dot_general(
                        piece, act, (((0,), (0,)), ((), ())),
                        preferred_element_type=jnp.float32,
                    )
                    term = lax.dot_general(
                        w_ref[k], piece, (((1,), (1,)), ((), ())),
                        preferred_element_type=jnp.float32,
                    )
                    if k == 0:
                        ag_ref[...] = term
                    else:
                        ag_ref[...] += term
        ag = ag_ref[...]
        dots = jnp.sum(ag * sx_ref[...], axis=0, keepdims=True)
        for j in range(n_chan):
            pk_ref[j, 0:block, :] = ag[j * block : (j + 1) * block]
            pk_ref[j, block : block + 1, :] = dots

    return pl.pallas_call(
        body,
        out_shape=(
            jax.ShapeDtypeStruct((27, outs, ins), jnp.float32),
            jax.ShapeDtypeStruct((n_chan, block + 1, cells), jnp.float32),
        ),
        in_specs=[pl.BlockSpec(memory_space=pltpu.VMEM)] * 4,
        out_specs=(
            pl.BlockSpec(memory_space=pltpu.VMEM),
            pl.BlockSpec(memory_space=pltpu.VMEM),
        ),
        scratch_shapes=[pltpu.VMEM((ins, cells), jnp.float32)],
        cost_estimate=pl.CostEstimate(
            flops=4 * 27 * ins * cells * outs,
            bytes_accessed=shifted.size * 2 + active_t.size * 2 + weight_t.size * 2
            + slope_x.size * 4 + 27 * ins * outs * 4 + (ins + n_chan) * cells * 4,
            transcendentals=0,
        ),
    )(shifted, active_t, weight_t, slope_x)


def halving_steps(axes):
    steps = []
    for axis in axes:
        size = lax.axis_size(axis)
        idx = lax.axis_index(axis)
        level = 1
        while level < size:
            steps.append((axis, level, (idx // level) % 2))
            level *= 2
    return steps


def exchange(block, axis, level):
    size = lax.axis_size(axis)
    return lax.ppermute(block, axis, [(i, i ^ level) for i in range(size)])


def halving_sum(x, steps):
    for axis, level, bit in steps:
        m = x.shape[0] // 2
        keep = lax.dynamic_slice_in_dim(x, bit * m, m, 0)
        send = lax.dynamic_slice_in_dim(x, (1 - bit) * m, m, 0)
        x = keep + exchange(send, axis, level)
    for axis, level, bit in reversed(steps):
        got = exchange(x, axis, level)
        x = lax.select_n(
            bit, jnp.concatenate([x, got], axis=0), jnp.concatenate([got, x], axis=0)
        )
    return x


def group_sum(x, near, far):
    near_steps, far_steps = halving_steps(near), halving_steps(far)
    unit = 2 ** (len(near_steps) + len(far_steps) + 1)
    rows = x.shape[0]
    padded_rows = -(-rows // unit) * unit
    x = jnp.pad(x, ((0, padded_rows - rows), (0, 0)))
    half = padded_rows // 2
    first = halving_sum(x[:half], near_steps + far_steps)
    second = halving_sum(x[half:], near_steps + far_steps[::-1])
    return jnp.concatenate([first, second], axis=0)[:rows]


def on_device(features, cotangent, conv_weight, norm_gain, norm_bias):
    chans, frames, rows, cols = features.shape
    n_chan = lax.axis_size("chan")
    whole_x = gather_blocks(features, "chan")
    total = whole_x.shape[0]
    cells = frames * rows * cols
    flat_x = whole_x.reshape(total, cells).astype(jnp.float32)
    inv_rms = lax.rsqrt(jnp.mean(flat_x * flat_x, axis=0, keepdims=True) + 1e-06)
    normed = flat_x * inv_rms * norm_gain[:, None] + norm_bias[:, None]
    active = jax.nn.silu(normed).astype(jnp.bfloat16).reshape(total, frames, rows, cols)

    ahead = from_behind(lax.slice_in_dim(cotangent, 0, 2, axis=1), "tm", -1)
    longer = jnp.concatenate([cotangent, ahead], axis=1)
    bordered = with_halo(longer, (("height", 2),), 1)
    padded = jnp.pad(bordered, ((0, 0), (0, 0), (0, 0), (1, 1)))

    positions = frames * lax.axis_size("tm") * rows * lax.axis_size("height") * cols
    cells_major = jnp.transpose(padded, (1, 2, 3, 0))
    shifted = jnp.stack(
        [cells_major[:, :, 2 - kw : 2 - kw + cols] for kw in range(3)], axis=0
    )
    active_t = jnp.transpose(active.reshape(total, cells))
    sig = jax.nn.sigmoid(normed)
    slope = sig * (1.0 + normed * (1.0 - sig)) * norm_gain[:, None]
    weight_t = jnp.transpose(conv_weight, (1, 2, 0))
    local_sums, packed = tap_kernel(
        shifted, active_t, weight_t, slope * flat_x, n_chan, frames, rows
    )
    summed = group_sum(local_sums.reshape(27 * chans, total), ("height",), ("tm",))
    weight_grad = jnp.transpose(
        (summed / math.sqrt(positions)).reshape(27, chans, total), (1, 0, 2)
    )

    mine = lax.psum_scatter(packed, "chan", scatter_dimension=0, tiled=True)[0]
    act_grad = mine[:chans]
    dots = mine[chans:]

    offset = lax.axis_index("chan") * chans
    own_x = features.reshape(chans, -1).astype(jnp.float32)
    own_slope = lax.dynamic_slice_in_dim(slope, offset, chans, 0)
    upstream = act_grad * own_slope
    own_back = inv_rms * upstream - own_x * inv_rms**3 * dots / total
    result = cotangent.reshape(chans, -1).astype(jnp.float32) + own_back
    return (result.astype(jnp.bfloat16).reshape(features.shape), weight_grad)


def solution(mesh):
    return jax.shard_map(
        on_device,
        mesh=mesh,
        in_specs=(
            P("chan", "tm", "height", None),
            P("chan", "tm", "height", None),
            P("chan", None, None),
            P(),
            P(),
        ),
        out_specs=(P("chan", "tm", "height", None), P("chan", None, None)),
        check_vma=False,
    )
```

```python
import math

import jax
import jax.numpy as jnp
from jax import lax
from jax.experimental import pallas as pl
from jax.experimental.pallas import tpu as pltpu
from jax.sharding import PartitionSpec as P


def from_behind(block, axis, distance):
    devices = range(lax.axis_size(axis))
    route = [(i - distance, i) for i in devices if i - distance in devices]
    return lax.ppermute(block, axis, route)


def with_halo(array, sides, width):
    for axis, dim in sides:
        size, length = (lax.axis_size(axis), array.shape[dim])
        up = [(i, (i + 1) % size) for i in range(size - 1)]
        down = [(j, i) for i, j in up]
        last = lax.slice_in_dim(array, length - width, length, axis=dim)
        first = lax.slice_in_dim(array, 0, width, axis=dim)
        before = lax.ppermute(last, axis, up)
        after = lax.ppermute(first, axis, down)
        array = jnp.concatenate([before, array, after], axis=dim)
    return array


def gather_blocks(block, axis):
    size = lax.axis_size(axis)
    me = lax.axis_index(axis)
    got = [block] + [
        lax.ppermute(block, axis, [(j, (j + d) % size) for j in range(size)])
        for d in range(1, size)
    ]
    return jnp.concatenate(
        [lax.select_n((me - j) % size, *got) for j in range(size)], axis=0
    )


def tap_kernel(shifted, active_t, weight_t, slope_x, n_chan, frames, rows, scale):
    _, _, _, cols, outs = shifted.shape
    cells, ins = active_t.shape
    block = ins // n_chan

    def body(cot_ref, act_ref, w_ref, sx_ref, wg_ref, pk_ref, ag_ref):
        act = act_ref[...]
        for kt in range(3):
            for kh in range(3):
                for kw in range(3):
                    k = 9 * kt + 3 * kh + kw
                    piece = cot_ref[kw, 2 - kt : 2 - kt + frames, 2 - kh : 2 - kh + rows]
                    piece = piece.reshape(cells, outs)
                    wg_ref[:, k, :] = scale * lax.dot_general(
                        piece, act, (((0,), (0,)), ((), ())),
                        preferred_element_type=jnp.float32,
                    )
                    term = lax.dot_general(
                        w_ref[k], piece, (((1,), (1,)), ((), ())),
                        preferred_element_type=jnp.float32,
                    )
                    if k == 0:
                        ag_ref[...] = term
                    else:
                        ag_ref[...] += term
        ag = ag_ref[...]
        dots = jnp.sum(ag * sx_ref[...], axis=0, keepdims=True)
        for j in range(n_chan):
            pk_ref[j, 0:block, :] = ag[j * block : (j + 1) * block]
            pk_ref[j, block : block + 1, :] = dots

    return pl.pallas_call(
        body,
        out_shape=(
            jax.ShapeDtypeStruct((outs, 27, ins), jnp.float32),
            jax.ShapeDtypeStruct((n_chan, block + 1, cells), jnp.float32),
        ),
        in_specs=[pl.BlockSpec(memory_space=pltpu.VMEM)] * 4,
        out_specs=(
            pl.BlockSpec(memory_space=pltpu.VMEM),
            pl.BlockSpec(memory_space=pltpu.VMEM),
        ),
        scratch_shapes=[pltpu.VMEM((ins, cells), jnp.float32)],
        cost_estimate=pl.CostEstimate(
            flops=4 * 27 * ins * cells * outs,
            bytes_accessed=shifted.size * 2 + active_t.size * 2 + weight_t.size * 2
            + slope_x.size * 4 + 27 * ins * outs * 4 + (ins + n_chan) * cells * 4,
            transcendentals=0,
        ),
    )(shifted, active_t, weight_t, slope_x)


def halving_steps(axes):
    steps = []
    for axis in axes:
        size = lax.axis_size(axis)
        idx = lax.axis_index(axis)
        level = 1
        while level < size:
            steps.append((axis, level, (idx // level) % 2))
            level *= 2
    return steps


def exchange(block, axis, level):
    size = lax.axis_size(axis)
    return lax.ppermute(block, axis, [(i, i ^ level) for i in range(size)])


def halving_sum(x, steps):
    for axis, level, bit in steps:
        m = x.shape[0] // 2
        keep = lax.dynamic_slice_in_dim(x, bit * m, m, 0)
        send = lax.dynamic_slice_in_dim(x, (1 - bit) * m, m, 0)
        x = keep + exchange(send, axis, level)
    for axis, level, bit in reversed(steps):
        got = exchange(x, axis, level)
        x = lax.select_n(
            bit, jnp.concatenate([x, got], axis=0), jnp.concatenate([got, x], axis=0)
        )
    return x


def group_sum(x, near, far):
    near_steps, far_steps = halving_steps(near), halving_steps(far)
    unit = 2 ** (len(near_steps) + len(far_steps) + 1)
    shape = x.shape
    if shape[0] % unit:
        x = x.reshape(shape[0] * shape[1], shape[2])
    rows = x.shape[0]
    padded_rows = -(-rows // unit) * unit
    x = jnp.pad(x, ((0, padded_rows - rows),) + ((0, 0),) * (x.ndim - 1))
    half = padded_rows // 2
    first = halving_sum(x[:half], near_steps + far_steps)
    second = halving_sum(x[half:], near_steps + far_steps[::-1])
    return jnp.concatenate([first, second], axis=0)[:rows].reshape(shape)


def on_device(features, cotangent, conv_weight, norm_gain, norm_bias):
    chans, frames, rows, cols = features.shape
    n_chan = lax.axis_size("chan")
    whole_x = gather_blocks(features, "chan")
    total = whole_x.shape[0]
    cells = frames * rows * cols
    flat_x = whole_x.reshape(total, cells).astype(jnp.float32)
    inv_rms = lax.rsqrt(jnp.mean(flat_x * flat_x, axis=0, keepdims=True) + 1e-06)
    normed = flat_x * inv_rms * norm_gain[:, None] + norm_bias[:, None]
    active = jax.nn.silu(normed).astype(jnp.bfloat16).reshape(total, frames, rows, cols)

    ahead = from_behind(lax.slice_in_dim(cotangent, 0, 2, axis=1), "tm", -1)
    longer = jnp.concatenate([cotangent, ahead], axis=1)
    bordered = with_halo(longer, (("height", 2),), 1)
    padded = jnp.pad(bordered, ((0, 0), (0, 0), (0, 0), (1, 1)))

    positions = frames * lax.axis_size("tm") * rows * lax.axis_size("height") * cols
    cells_major = jnp.transpose(padded, (1, 2, 3, 0))
    shifted = jnp.stack(
        [cells_major[:, :, 2 - kw : 2 - kw + cols] for kw in range(3)], axis=0
    )
    active_t = jnp.transpose(active.reshape(total, cells))
    sig = jax.nn.sigmoid(normed)
    slope = sig * (1.0 + normed * (1.0 - sig)) * norm_gain[:, None]
    weight_t = jnp.transpose(conv_weight, (1, 2, 0))
    local_sums, packed = tap_kernel(
        shifted, active_t, weight_t, slope * flat_x, n_chan, frames, rows,
        1.0 / math.sqrt(positions),
    )
    weight_grad = group_sum(local_sums, ("height",), ("tm",))

    mine = lax.psum_scatter(packed, "chan", scatter_dimension=0, tiled=True)[0]
    act_grad = mine[:chans]
    dots = mine[chans:]

    offset = lax.axis_index("chan") * chans
    own_x = features.reshape(chans, -1).astype(jnp.float32)
    own_slope = lax.dynamic_slice_in_dim(slope, offset, chans, 0)
    upstream = act_grad * own_slope
    own_back = inv_rms * upstream - own_x * inv_rms**3 * dots / total
    result = cotangent.reshape(chans, -1).astype(jnp.float32) + own_back
    return (result.astype(jnp.bfloat16).reshape(features.shape), weight_grad)


def solution(mesh):
    return jax.shard_map(
        on_device,
        mesh=mesh,
        in_specs=(
            P("chan", "tm", "height", None),
            P("chan", "tm", "height", None),
            P("chan", None, None),
            P(),
            P(),
        ),
        out_specs=(P("chan", "tm", "height", None), P("chan", None, None)),
        check_vma=False,
    )
```

```python
import math

import jax
import jax.numpy as jnp
from jax import lax
from jax.experimental import pallas as pl
from jax.experimental.pallas import tpu as pltpu
from jax.sharding import PartitionSpec as P


def from_behind(block, axis, distance):
    devices = range(lax.axis_size(axis))
    route = [(i - distance, i) for i in devices if i - distance in devices]
    return lax.ppermute(block, axis, route)


def with_halo(array, sides, width):
    for axis, dim in sides:
        size, length = (lax.axis_size(axis), array.shape[dim])
        up = [(i, (i + 1) % size) for i in range(size - 1)]
        down = [(j, i) for i, j in up]
        last = lax.slice_in_dim(array, length - width, length, axis=dim)
        first = lax.slice_in_dim(array, 0, width, axis=dim)
        before = lax.ppermute(last, axis, up)
        after = lax.ppermute(first, axis, down)
        array = jnp.concatenate([before, array, after], axis=dim)
    return array


def gather_blocks(block, axis):
    size = lax.axis_size(axis)
    me = lax.axis_index(axis)
    got = [block] + [
        lax.ppermute(block, axis, [(j, (j + d) % size) for j in range(size)])
        for d in range(1, size)
    ]
    return jnp.concatenate(
        [lax.select_n((me - j) % size, *got) for j in range(size)], axis=0
    )


def weight_taps(shifted, active_t, frames, rows):
    _, _, _, cols, outs = shifted.shape
    cells, ins = active_t.shape

    def body(cot_ref, act_ref, wg_ref):
        act = act_ref[...]
        for kt in range(3):
            for kh in range(3):
                for kw in range(3):
                    piece = cot_ref[kw, 2 - kt : 2 - kt + frames, 2 - kh : 2 - kh + rows]
                    wg_ref[9 * kt + 3 * kh + kw] = lax.dot_general(
                        piece.reshape(cells, outs), act, (((0,), (0,)), ((), ())),
                        preferred_element_type=jnp.float32,
                    )

    return pl.pallas_call(
        body,
        out_shape=jax.ShapeDtypeStruct((27, outs, ins), jnp.float32),
        in_specs=[pl.BlockSpec(memory_space=pltpu.VMEM)] * 2,
        out_specs=pl.BlockSpec(memory_space=pltpu.VMEM),
        cost_estimate=pl.CostEstimate(
            flops=2 * 27 * ins * cells * outs,
            bytes_accessed=shifted.size * 2 + active_t.size * 2 + 27 * ins * outs * 4,
            transcendentals=0,
        ),
    )(shifted, active_t)


def act_taps(shifted, weight_t, slope_x, anchor, n_chan, frames, rows):
    _, _, _, cols, outs = shifted.shape
    ins, cells = slope_x.shape
    block = ins // n_chan

    def body(cot_ref, w_ref, sx_ref, anchor_ref, pk_ref, ag_ref):
        for kt in range(3):
            for kh in range(3):
                for kw in range(3):
                    k = 9 * kt + 3 * kh + kw
                    piece = cot_ref[kw, 2 - kt : 2 - kt + frames, 2 - kh : 2 - kh + rows]
                    term = lax.dot_general(
                        w_ref[k], piece.reshape(cells, outs), (((1,), (1,)), ((), ())),
                        preferred_element_type=jnp.float32,
                    )
                    if k == 0:
                        ag_ref[...] = term
                    else:
                        ag_ref[...] += term
        ag = ag_ref[...]
        dots = jnp.sum(ag * sx_ref[...], axis=0, keepdims=True)
        for j in range(n_chan):
            pk_ref[j, 0:block, :] = ag[j * block : (j + 1) * block]
            pk_ref[j, block : block + 1, :] = dots

    return pl.pallas_call(
        body,
        out_shape=jax.ShapeDtypeStruct((n_chan, block + 1, cells), jnp.float32),
        in_specs=[pl.BlockSpec(memory_space=pltpu.VMEM)] * 4,
        out_specs=pl.BlockSpec(memory_space=pltpu.VMEM),
        scratch_shapes=[pltpu.VMEM((ins, cells), jnp.float32)],
        cost_estimate=pl.CostEstimate(
            flops=2 * 27 * ins * cells * outs,
            bytes_accessed=shifted.size * 2 + weight_t.size * 2 + slope_x.size * 4
            + (ins + n_chan) * cells * 4,
            transcendentals=0,
        ),
    )(shifted, weight_t, slope_x, anchor)


def halving_steps(axes):
    steps = []
    for axis in axes:
        size = lax.axis_size(axis)
        idx = lax.axis_index(axis)
        level = 1
        while level < size:
            steps.append((axis, level, (idx // level) % 2))
            level *= 2
    return steps


def exchange(block, axis, level):
    size = lax.axis_size(axis)
    return lax.ppermute(block, axis, [(i, i ^ level) for i in range(size)])


def halving_sum(x, steps):
    for axis, level, bit in steps:
        m = x.shape[0] // 2
        keep = lax.dynamic_slice_in_dim(x, bit * m, m, 0)
        send = lax.dynamic_slice_in_dim(x, (1 - bit) * m, m, 0)
        x = keep + exchange(send, axis, level)
    for axis, level, bit in reversed(steps):
        got = exchange(x, axis, level)
        x = lax.select_n(
            bit, jnp.concatenate([x, got], axis=0), jnp.concatenate([got, x], axis=0)
        )
    return x


def group_sum(x, near, far):
    near_steps, far_steps = halving_steps(near), halving_steps(far)
    unit = 2 ** (len(near_steps) + len(far_steps) + 1)
    rows = x.shape[0]
    padded_rows = -(-rows // unit) * unit
    x = jnp.pad(x, ((0, padded_rows - rows), (0, 0)))
    half = padded_rows // 2
    first = halving_sum(x[:half], near_steps + far_steps)
    second = halving_sum(x[half:], near_steps + far_steps[::-1])
    return jnp.concatenate([first, second], axis=0)[:rows]


def on_device(features, cotangent, conv_weight, norm_gain, norm_bias):
    chans, frames, rows, cols = features.shape
    n_chan = lax.axis_size("chan")
    whole_x = gather_blocks(features, "chan")
    total = whole_x.shape[0]
    cells = frames * rows * cols
    flat_x = whole_x.reshape(total, cells).astype(jnp.float32)
    inv_rms = lax.rsqrt(jnp.mean(flat_x * flat_x, axis=0, keepdims=True) + 1e-06)
    normed = flat_x * inv_rms * norm_gain[:, None] + norm_bias[:, None]
    active = jax.nn.silu(normed).astype(jnp.bfloat16).reshape(total, frames, rows, cols)

    ahead = from_behind(lax.slice_in_dim(cotangent, 0, 2, axis=1), "tm", -1)
    longer = jnp.concatenate([cotangent, ahead], axis=1)
    bordered = with_halo(longer, (("height", 2),), 1)
    padded = jnp.pad(bordered, ((0, 0), (0, 0), (0, 0), (1, 1)))

    positions = frames * lax.axis_size("tm") * rows * lax.axis_size("height") * cols
    cells_major = jnp.transpose(padded, (1, 2, 3, 0))
    shifted = jnp.stack(
        [cells_major[:, :, 2 - kw : 2 - kw + cols] for kw in range(3)], axis=0
    )
    active_t = jnp.transpose(active.reshape(total, cells))
    sig = jax.nn.sigmoid(normed)
    slope = sig * (1.0 + normed * (1.0 - sig)) * norm_gain[:, None]
    weight_t = jnp.transpose(conv_weight, (1, 2, 0))
    local_sums = weight_taps(shifted, active_t, frames, rows)
    packed = act_taps(
        shifted, weight_t, slope * flat_x, local_sums[0, :8, :128], n_chan, frames, rows
    )
    summed = group_sum(local_sums.reshape(27 * chans, total), ("height",), ("tm",))
    weight_grad = jnp.transpose(
        (summed / math.sqrt(positions)).reshape(27, chans, total), (1, 0, 2)
    )

    mine = lax.psum_scatter(packed, "chan", scatter_dimension=0, tiled=True)[0]
    act_grad = mine[:chans]
    dots = mine[chans:]

    offset = lax.axis_index("chan") * chans
    own_x = features.reshape(chans, -1).astype(jnp.float32)
    own_slope = lax.dynamic_slice_in_dim(slope, offset, chans, 0)
    upstream = act_grad * own_slope
    own_back = inv_rms * upstream - own_x * inv_rms**3 * dots / total
    result = cotangent.reshape(chans, -1).astype(jnp.float32) + own_back
    return (result.astype(jnp.bfloat16).reshape(features.shape), weight_grad)


def solution(mesh):
    return jax.shard_map(
        on_device,
        mesh=mesh,
        in_specs=(
            P("chan", "tm", "height", None),
            P("chan", "tm", "height", None),
            P("chan", None, None),
            P(),
            P(),
        ),
        out_specs=(P("chan", "tm", "height", None), P("chan", None, None)),
        check_vma=False,
    )
```

```python
import math

import jax
import jax.numpy as jnp
from jax import lax
from jax.experimental import pallas as pl
from jax.experimental.pallas import tpu as pltpu
from jax.sharding import PartitionSpec as P


def from_behind(block, axis, distance):
    devices = range(lax.axis_size(axis))
    route = [(i - distance, i) for i in devices if i - distance in devices]
    return lax.ppermute(block, axis, route)


def with_halo(array, sides, width):
    for axis, dim in sides:
        size, length = (lax.axis_size(axis), array.shape[dim])
        up = [(i, (i + 1) % size) for i in range(size - 1)]
        down = [(j, i) for i, j in up]
        last = lax.slice_in_dim(array, length - width, length, axis=dim)
        first = lax.slice_in_dim(array, 0, width, axis=dim)
        before = lax.ppermute(last, axis, up)
        after = lax.ppermute(first, axis, down)
        array = jnp.concatenate([before, array, after], axis=dim)
    return array


def gather_blocks(block, axis):
    size = lax.axis_size(axis)
    me = lax.axis_index(axis)
    got = [block] + [
        lax.ppermute(block, axis, [(j, (j + d) % size) for j in range(size)])
        for d in range(1, size)
    ]
    return jnp.concatenate(
        [lax.select_n((me - j) % size, *got) for j in range(size)], axis=0
    )


def weight_taps(shifted, active_t, frames, rows):
    _, _, _, cols, outs = shifted.shape
    cells, ins = active_t.shape

    def body(cot_ref, act_ref, wg_ref):
        act = act_ref[...]
        for kt in range(3):
            for kh in range(3):
                for kw in range(3):
                    piece = cot_ref[kw, 2 - kt : 2 - kt + frames, 2 - kh : 2 - kh + rows]
                    wg_ref[9 * kt + 3 * kh + kw] = lax.dot_general(
                        piece.reshape(cells, outs), act, (((0,), (0,)), ((), ())),
                        preferred_element_type=jnp.float32,
                    )

    return pl.pallas_call(
        body,
        out_shape=jax.ShapeDtypeStruct((27, outs, ins), jnp.float32),
        in_specs=[pl.BlockSpec(memory_space=pltpu.VMEM)] * 2,
        out_specs=pl.BlockSpec(memory_space=pltpu.VMEM),
        cost_estimate=pl.CostEstimate(
            flops=2 * 27 * ins * cells * outs,
            bytes_accessed=shifted.size * 2 + active_t.size * 2 + 27 * ins * outs * 4,
            transcendentals=0,
        ),
    )(shifted, active_t)


def act_taps(shifted, weight_t, frames, rows):
    _, _, _, cols, outs = shifted.shape
    _, ins, _ = weight_t.shape
    cells = frames * rows * cols

    def body(cot_ref, w_ref, ag_ref):
        for kt in range(3):
            for kh in range(3):
                for kw in range(3):
                    k = 9 * kt + 3 * kh + kw
                    piece = cot_ref[kw, 2 - kt : 2 - kt + frames, 2 - kh : 2 - kh + rows]
                    term = lax.dot_general(
                        w_ref[k], piece.reshape(cells, outs), (((1,), (1,)), ((), ())),
                        preferred_element_type=jnp.float32,
                    )
                    if k == 0:
                        ag_ref[...] = term
                    else:
                        ag_ref[...] += term

    return pl.pallas_call(
        body,
        out_shape=jax.ShapeDtypeStruct((ins, cells), jnp.float32),
        in_specs=[pl.BlockSpec(memory_space=pltpu.VMEM)] * 2,
        out_specs=pl.BlockSpec(memory_space=pltpu.VMEM),
        cost_estimate=pl.CostEstimate(
            flops=2 * 27 * ins * cells * outs,
            bytes_accessed=shifted.size * 2 + weight_t.size * 2 + ins * cells * 4,
            transcendentals=0,
        ),
    )(shifted, weight_t)


def halving_steps(axes):
    steps = []
    for axis in axes:
        size = lax.axis_size(axis)
        idx = lax.axis_index(axis)
        level = 1
        while level < size:
            steps.append((axis, level, (idx // level) % 2))
            level *= 2
    return steps


def exchange(block, axis, level):
    size = lax.axis_size(axis)
    return lax.ppermute(block, axis, [(i, i ^ level) for i in range(size)])


def halving_sum(x, steps):
    for axis, level, bit in steps:
        m = x.shape[0] // 2
        keep = lax.dynamic_slice_in_dim(x, bit * m, m, 0)
        send = lax.dynamic_slice_in_dim(x, (1 - bit) * m, m, 0)
        x = keep + exchange(send, axis, level)
    for axis, level, bit in reversed(steps):
        got = exchange(x, axis, level)
        x = lax.select_n(
            bit, jnp.concatenate([x, got], axis=0), jnp.concatenate([got, x], axis=0)
        )
    return x


def group_sum(x, near, far):
    near_steps, far_steps = halving_steps(near), halving_steps(far)
    unit = 2 ** (len(near_steps) + len(far_steps) + 1)
    rows = x.shape[0]
    padded_rows = -(-rows // unit) * unit
    x = jnp.pad(x, ((0, padded_rows - rows), (0, 0)))
    half = padded_rows // 2
    first = halving_sum(x[:half], near_steps + far_steps)
    second = halving_sum(x[half:], near_steps + far_steps[::-1])
    return jnp.concatenate([first, second], axis=0)[:rows]


def on_device(features, cotangent, conv_weight, norm_gain, norm_bias):
    chans, frames, rows, cols = features.shape
    n_chan = lax.axis_size("chan")
    ahead = from_behind(lax.slice_in_dim(cotangent, 0, 2, axis=1), "tm", -1)
    longer = jnp.concatenate([cotangent, ahead], axis=1)
    bordered = with_halo(longer, (("height", 2),), 1)
    padded = jnp.pad(bordered, ((0, 0), (0, 0), (0, 0), (1, 1)))

    cells_major = jnp.transpose(padded, (1, 2, 3, 0))
    shifted = jnp.stack(
        [cells_major[:, :, 2 - kw : 2 - kw + cols] for kw in range(3)], axis=0
    )
    weight_t = jnp.transpose(conv_weight, (1, 2, 0))
    partial = act_taps(shifted, weight_t, frames, rows)

    held, _ = lax.optimization_barrier((features, padded))
    whole_x = gather_blocks(held, "chan")
    total = whole_x.shape[0]
    cells = frames * rows * cols
    flat_x = whole_x.reshape(total, cells).astype(jnp.float32)
    inv_rms = lax.rsqrt(jnp.mean(flat_x * flat_x, axis=0, keepdims=True) + 1e-06)
    normed = flat_x * inv_rms * norm_gain[:, None] + norm_bias[:, None]
    active = jax.nn.silu(normed).astype(jnp.bfloat16).reshape(total, frames, rows, cols)

    positions = frames * lax.axis_size("tm") * rows * lax.axis_size("height") * cols
    active_t = jnp.transpose(active.reshape(total, cells))
    sig = jax.nn.sigmoid(normed)
    slope = sig * (1.0 + normed * (1.0 - sig)) * norm_gain[:, None]
    part_dots = jnp.sum(partial * slope * flat_x, axis=0, keepdims=True)
    packed = jnp.concatenate(
        [
            partial.reshape(n_chan, chans, cells),
            jnp.broadcast_to(part_dots[None], (n_chan, 1, cells)),
        ],
        axis=1,
    )
    local_sums = weight_taps(shifted, active_t, frames, rows)
    summed = group_sum(local_sums.reshape(27 * chans, total), ("height",), ("tm",))
    weight_grad = jnp.transpose(
        (summed / math.sqrt(positions)).reshape(27, chans, total), (1, 0, 2)
    )

    mine = lax.psum_scatter(packed, "chan", scatter_dimension=0, tiled=True)[0]
    act_grad = mine[:chans]
    dots = mine[chans:]

    offset = lax.axis_index("chan") * chans
    own_x = features.reshape(chans, -1).astype(jnp.float32)
    own_slope = lax.dynamic_slice_in_dim(slope, offset, chans, 0)
    upstream = act_grad * own_slope
    own_back = inv_rms * upstream - own_x * inv_rms**3 * dots / total
    result = cotangent.reshape(chans, -1).astype(jnp.float32) + own_back
    return (result.astype(jnp.bfloat16).reshape(features.shape), weight_grad)


def solution(mesh):
    return jax.shard_map(
        on_device,
        mesh=mesh,
        in_specs=(
            P("chan", "tm", "height", None),
            P("chan", "tm", "height", None),
            P("chan", None, None),
            P(),
            P(),
        ),
        out_specs=(P("chan", "tm", "height", None), P("chan", None, None)),
        check_vma=False,
    )
```

```python
import math

import jax
import jax.numpy as jnp
from jax import lax
from jax.experimental import pallas as pl
from jax.experimental.pallas import tpu as pltpu
from jax.sharding import PartitionSpec as P


def from_behind(block, axis, distance):
    devices = range(lax.axis_size(axis))
    route = [(i - distance, i) for i in devices if i - distance in devices]
    return lax.ppermute(block, axis, route)


def with_halo(array, sides, width):
    for axis, dim in sides:
        size, length = (lax.axis_size(axis), array.shape[dim])
        up = [(i, (i + 1) % size) for i in range(size - 1)]
        down = [(j, i) for i, j in up]
        last = lax.slice_in_dim(array, length - width, length, axis=dim)
        first = lax.slice_in_dim(array, 0, width, axis=dim)
        before = lax.ppermute(last, axis, up)
        after = lax.ppermute(first, axis, down)
        array = jnp.concatenate([before, array, after], axis=dim)
    return array


def gather_blocks(block, axis):
    size = lax.axis_size(axis)
    me = lax.axis_index(axis)
    got = [block] + [
        lax.ppermute(block, axis, [(j, (j + d) % size) for j in range(size)])
        for d in range(1, size)
    ]
    return jnp.concatenate(
        [lax.select_n((me - j) % size, *got) for j in range(size)], axis=0
    )


def tap_kernel(shifted, active_t, weight_t, slope_x, n_chan, frames, rows):
    _, _, _, cols, outs = shifted.shape
    cells, ins = active_t.shape
    block = ins // n_chan

    def body(cot_ref, act_ref, w_ref, sx_ref, wg_ref, pk_ref, ag_ref):
        act = act_ref[...]
        for kt in range(3):
            for kh in range(3):
                for kw in range(3):
                    k = 9 * kt + 3 * kh + kw
                    piece = cot_ref[kw, 2 - kt : 2 - kt + frames, 2 - kh : 2 - kh + rows]
                    piece = piece.reshape(cells, outs)
                    wg_ref[k] = lax.dot_general(
                        piece, act, (((0,), (0,)), ((), ())),
                        preferred_element_type=jnp.float32,
                    )
                    term = lax.dot_general(
                        w_ref[k], piece, (((1,), (1,)), ((), ())),
                        preferred_element_type=jnp.float32,
                    )
                    if k == 0:
                        ag_ref[...] = term
                    else:
                        ag_ref[...] += term
        ag = ag_ref[...]
        dots = jnp.sum(ag * sx_ref[...], axis=0, keepdims=True)
        for j in range(n_chan):
            pk_ref[j, 0:block, :] = ag[j * block : (j + 1) * block]
            pk_ref[j, block : block + 1, :] = dots

    return pl.pallas_call(
        body,
        out_shape=(
            jax.ShapeDtypeStruct((27, outs, ins), jnp.float32),
            jax.ShapeDtypeStruct((n_chan, block + 1, cells), jnp.float32),
        ),
        in_specs=[pl.BlockSpec(memory_space=pltpu.VMEM)] * 4,
        out_specs=(
            pl.BlockSpec(memory_space=pltpu.VMEM),
            pl.BlockSpec(memory_space=pltpu.VMEM),
        ),
        scratch_shapes=[pltpu.VMEM((ins, cells), jnp.float32)],
        cost_estimate=pl.CostEstimate(
            flops=4 * 27 * ins * cells * outs,
            bytes_accessed=shifted.size * 2 + active_t.size * 2 + weight_t.size * 2
            + slope_x.size * 4 + 27 * ins * outs * 4 + (ins + n_chan) * cells * 4,
            transcendentals=0,
        ),
    )(shifted, active_t, weight_t, slope_x)


def halving_steps(axes):
    steps = []
    for axis in axes:
        size = lax.axis_size(axis)
        idx = lax.axis_index(axis)
        level = 1
        while level < size:
            steps.append((axis, level, (idx // level) % 2))
            level *= 2
    return steps


def exchange(block, axis, level):
    size = lax.axis_size(axis)
    return lax.ppermute(block, axis, [(i, i ^ level) for i in range(size)])


def halving_sum(x, steps):
    for axis, level, bit in steps:
        m = x.shape[0] // 2
        keep = lax.dynamic_slice_in_dim(x, bit * m, m, 0)
        send = lax.dynamic_slice_in_dim(x, (1 - bit) * m, m, 0)
        x = keep + exchange(send, axis, level)
    for axis, level, bit in reversed(steps[1:]):
        got = exchange(x, axis, level)
        x = lax.select_n(
            bit, jnp.concatenate([x, got], axis=0), jnp.concatenate([got, x], axis=0)
        )
    axis, level, bit = steps[0]
    return x, exchange(x, axis, level), bit


def group_sum(x, near, far):
    near_steps, far_steps = halving_steps(near), halving_steps(far)
    unit = 2 ** (len(near_steps) + len(far_steps) + 1)
    rows = x.shape[0]
    padded_rows = -(-rows // unit) * unit
    x = jnp.pad(x, ((0, padded_rows - rows), (0, 0)))
    half = padded_rows // 2
    mine1, got1, bit = halving_sum(x[:half], near_steps + far_steps)
    mine2, got2, _ = halving_sum(x[half:], near_steps + far_steps[::-1])
    both = lax.select_n(
        bit,
        jnp.concatenate([mine1, got1, mine2, got2], axis=0),
        jnp.concatenate([got1, mine1, got2, mine2], axis=0),
    )
    return both[:rows]


def on_device(features, cotangent, conv_weight, norm_gain, norm_bias):
    chans, frames, rows, cols = features.shape
    n_chan = lax.axis_size("chan")
    whole_x = gather_blocks(features, "chan")
    total = whole_x.shape[0]
    cells = frames * rows * cols
    flat_x = whole_x.reshape(total, cells).astype(jnp.float32)
    inv_rms = lax.rsqrt(jnp.mean(flat_x * flat_x, axis=0, keepdims=True) + 1e-06)
    normed = flat_x * inv_rms * norm_gain[:, None] + norm_bias[:, None]
    active = jax.nn.silu(normed).astype(jnp.bfloat16).reshape(total, frames, rows, cols)

    ahead = from_behind(lax.slice_in_dim(cotangent, 0, 2, axis=1), "tm", -1)
    longer = jnp.concatenate([cotangent, ahead], axis=1)
    bordered = with_halo(longer, (("height", 2),), 1)
    padded = jnp.pad(bordered, ((0, 0), (0, 0), (0, 0), (1, 1)))

    positions = frames * lax.axis_size("tm") * rows * lax.axis_size("height") * cols
    cells_major = jnp.transpose(padded, (1, 2, 3, 0))
    shifted = jnp.stack(
        [cells_major[:, :, 2 - kw : 2 - kw + cols] for kw in range(3)], axis=0
    )
    active_t = jnp.transpose(active.reshape(total, cells))
    sig = jax.nn.sigmoid(normed)
    slope = sig * (1.0 + normed * (1.0 - sig)) * norm_gain[:, None]
    weight_t = jnp.transpose(conv_weight, (1, 2, 0))
    local_sums, packed = tap_kernel(
        shifted, active_t, weight_t, slope * flat_x, n_chan, frames, rows
    )
    summed = group_sum(local_sums.reshape(27 * chans, total), ("height",), ("tm",))
    weight_grad = jnp.transpose(
        (summed / math.sqrt(positions)).reshape(27, chans, total), (1, 0, 2)
    )

    mine = lax.psum_scatter(packed, "chan", scatter_dimension=0, tiled=True)[0]
    act_grad = mine[:chans]
    dots = mine[chans:]

    offset = lax.axis_index("chan") * chans
    own_x = features.reshape(chans, -1).astype(jnp.float32)
    own_slope = lax.dynamic_slice_in_dim(slope, offset, chans, 0)
    upstream = act_grad * own_slope
    own_back = inv_rms * upstream - own_x * inv_rms**3 * dots / total
    result = cotangent.reshape(chans, -1).astype(jnp.float32) + own_back
    return (result.astype(jnp.bfloat16).reshape(features.shape), weight_grad)


def solution(mesh):
    return jax.shard_map(
        on_device,
        mesh=mesh,
        in_specs=(
            P("chan", "tm", "height", None),
            P("chan", "tm", "height", None),
            P("chan", None, None),
            P(),
            P(),
        ),
        out_specs=(P("chan", "tm", "height", None), P("chan", None, None)),
        check_vma=False,
    )
```

```python
import math

import jax
import jax.numpy as jnp
from jax import lax
from jax.experimental import pallas as pl
from jax.experimental.pallas import tpu as pltpu
from jax.sharding import PartitionSpec as P


def from_behind(block, axis, distance):
    devices = range(lax.axis_size(axis))
    route = [(i - distance, i) for i in devices if i - distance in devices]
    return lax.ppermute(block, axis, route)


def with_halo(array, sides, width):
    for axis, dim in sides:
        size, length = (lax.axis_size(axis), array.shape[dim])
        last = lax.slice_in_dim(array, length - width, length, axis=dim)
        first = lax.slice_in_dim(array, 0, width, axis=dim)
        if size == 2:
            me = lax.axis_index(axis)
            got = lax.ppermute(lax.select_n(me, last, first), axis, [(0, 1), (1, 0)])
            zero = jnp.zeros_like(got)
            before = lax.select_n(me, zero, got)
            after = lax.select_n(me, got, zero)
        else:
            up = [(i, (i + 1) % size) for i in range(size - 1)]
            down = [(j, i) for i, j in up]
            before = lax.ppermute(last, axis, up)
            after = lax.ppermute(first, axis, down)
        array = jnp.concatenate([before, array, after], axis=dim)
    return array


def gather_blocks(block, axis):
    size = lax.axis_size(axis)
    me = lax.axis_index(axis)
    got = [block] + [
        lax.ppermute(block, axis, [(j, (j + d) % size) for j in range(size)])
        for d in range(1, size)
    ]
    return jnp.concatenate(
        [lax.select_n((me - j) % size, *got) for j in range(size)], axis=0
    )


def tap_kernel(shifted, active_t, weight_t, slope_x, n_chan, frames, rows):
    _, _, _, cols, outs = shifted.shape
    cells, ins = active_t.shape
    block = ins // n_chan

    def body(cot_ref, act_ref, w_ref, sx_ref, wg_ref, pk_ref, ag_ref):
        act = act_ref[...]
        for kt in range(3):
            for kh in range(3):
                for kw in range(3):
                    k = 9 * kt + 3 * kh + kw
                    piece = cot_ref[kw, 2 - kt : 2 - kt + frames, 2 - kh : 2 - kh + rows]
                    piece = piece.reshape(cells, outs)
                    wg_ref[k] = lax.dot_general(
                        piece, act, (((0,), (0,)), ((), ())),
                        preferred_element_type=jnp.float32,
                    )
                    term = lax.dot_general(
                        w_ref[k], piece, (((1,), (1,)), ((), ())),
                        preferred_element_type=jnp.float32,
                    )
                    if k == 0:
                        ag_ref[...] = term
                    else:
                        ag_ref[...] += term
        ag = ag_ref[...]
        dots = jnp.sum(ag * sx_ref[...], axis=0, keepdims=True)
        for j in range(n_chan):
            pk_ref[j, 0:block, :] = ag[j * block : (j + 1) * block]
            pk_ref[j, block : block + 1, :] = dots

    return pl.pallas_call(
        body,
        out_shape=(
            jax.ShapeDtypeStruct((27, outs, ins), jnp.float32),
            jax.ShapeDtypeStruct((n_chan, block + 1, cells), jnp.float32),
        ),
        in_specs=[pl.BlockSpec(memory_space=pltpu.VMEM)] * 4,
        out_specs=(
            pl.BlockSpec(memory_space=pltpu.VMEM),
            pl.BlockSpec(memory_space=pltpu.VMEM),
        ),
        scratch_shapes=[pltpu.VMEM((ins, cells), jnp.float32)],
        cost_estimate=pl.CostEstimate(
            flops=4 * 27 * ins * cells * outs,
            bytes_accessed=shifted.size * 2 + active_t.size * 2 + weight_t.size * 2
            + slope_x.size * 4 + 27 * ins * outs * 4 + (ins + n_chan) * cells * 4,
            transcendentals=0,
        ),
    )(shifted, active_t, weight_t, slope_x)


def halving_steps(axes):
    steps = []
    for axis in axes:
        size = lax.axis_size(axis)
        idx = lax.axis_index(axis)
        level = 1
        while level < size:
            steps.append((axis, level, (idx // level) % 2))
            level *= 2
    return steps


def exchange(block, axis, level):
    size = lax.axis_size(axis)
    return lax.ppermute(block, axis, [(i, i ^ level) for i in range(size)])


def halving_sum(x, steps):
    for axis, level, bit in steps:
        m = x.shape[0] // 2
        keep = lax.dynamic_slice_in_dim(x, bit * m, m, 0)
        send = lax.dynamic_slice_in_dim(x, (1 - bit) * m, m, 0)
        x = keep + exchange(send, axis, level)
    for axis, level, bit in reversed(steps[1:]):
        got = exchange(x, axis, level)
        x = lax.select_n(
            bit, jnp.concatenate([x, got], axis=0), jnp.concatenate([got, x], axis=0)
        )
    axis, level, bit = steps[0]
    return x, exchange(x, axis, level), bit


def group_sum(x, near, far):
    near_steps, far_steps = halving_steps(near), halving_steps(far)
    unit = 2 ** (len(near_steps) + len(far_steps) + 1)
    rows = x.shape[0]
    padded_rows = -(-rows // unit) * unit
    x = jnp.pad(x, ((0, padded_rows - rows), (0, 0)))
    half = padded_rows // 2
    mine1, got1, bit = halving_sum(x[:half], near_steps + far_steps)
    mine2, got2, _ = halving_sum(x[half:], near_steps + far_steps[::-1])
    both = lax.select_n(
        bit,
        jnp.concatenate([mine1, got1, mine2, got2], axis=0),
        jnp.concatenate([got1, mine1, got2, mine2], axis=0),
    )
    return both[:rows]


def on_device(features, cotangent, conv_weight, norm_gain, norm_bias):
    chans, frames, rows, cols = features.shape
    n_chan = lax.axis_size("chan")
    whole_x = gather_blocks(features, "chan")
    total = whole_x.shape[0]
    cells = frames * rows * cols
    flat_x = whole_x.reshape(total, cells).astype(jnp.float32)
    inv_rms = lax.rsqrt(jnp.mean(flat_x * flat_x, axis=0, keepdims=True) + 1e-06)
    normed = flat_x * inv_rms * norm_gain[:, None] + norm_bias[:, None]
    active = jax.nn.silu(normed).astype(jnp.bfloat16).reshape(total, frames, rows, cols)

    ahead = from_behind(lax.slice_in_dim(cotangent, 0, 2, axis=1), "tm", -1)
    longer = jnp.concatenate([cotangent, ahead], axis=1)
    bordered = with_halo(longer, (("height", 2),), 1)
    padded = jnp.pad(bordered, ((0, 0), (0, 0), (0, 0), (1, 1)))

    positions = frames * lax.axis_size("tm") * rows * lax.axis_size("height") * cols
    cells_major = jnp.transpose(padded, (1, 2, 3, 0))
    shifted = jnp.stack(
        [cells_major[:, :, 2 - kw : 2 - kw + cols] for kw in range(3)], axis=0
    )
    active_t = jnp.transpose(active.reshape(total, cells))
    sig = jax.nn.sigmoid(normed)
    slope = sig * (1.0 + normed * (1.0 - sig)) * norm_gain[:, None]
    weight_t = jnp.transpose(conv_weight, (1, 2, 0))
    local_sums, packed = tap_kernel(
        shifted, active_t, weight_t, slope * flat_x, n_chan, frames, rows
    )
    summed = group_sum(local_sums.reshape(27 * chans, total), ("height",), ("tm",))
    weight_grad = jnp.transpose(
        (summed / math.sqrt(positions)).reshape(27, chans, total), (1, 0, 2)
    )

    mine = lax.psum_scatter(packed, "chan", scatter_dimension=0, tiled=True)[0]
    act_grad = mine[:chans]
    dots = mine[chans:]

    offset = lax.axis_index("chan") * chans
    own_x = features.reshape(chans, -1).astype(jnp.float32)
    own_slope = lax.dynamic_slice_in_dim(slope, offset, chans, 0)
    upstream = act_grad * own_slope
    own_back = inv_rms * upstream - own_x * inv_rms**3 * dots / total
    result = cotangent.reshape(chans, -1).astype(jnp.float32) + own_back
    return (result.astype(jnp.bfloat16).reshape(features.shape), weight_grad)


def solution(mesh):
    return jax.shard_map(
        on_device,
        mesh=mesh,
        in_specs=(
            P("chan", "tm", "height", None),
            P("chan", "tm", "height", None),
            P("chan", None, None),
            P(),
            P(),
        ),
        out_specs=(P("chan", "tm", "height", None), P("chan", None, None)),
        check_vma=False,
    )
```

```python
import math

import jax
import jax.numpy as jnp
from jax import lax
from jax.experimental import pallas as pl
from jax.experimental.pallas import tpu as pltpu
from jax.sharding import PartitionSpec as P


def from_behind(block, axis, distance):
    devices = range(lax.axis_size(axis))
    route = [(i - distance, i) for i in devices if i - distance in devices]
    return lax.ppermute(block, axis, route)


def with_halo(array, sides, width):
    for axis, dim in sides:
        size, length = (lax.axis_size(axis), array.shape[dim])
        last = lax.slice_in_dim(array, length - width, length, axis=dim)
        first = lax.slice_in_dim(array, 0, width, axis=dim)
        if size == 2:
            me = lax.axis_index(axis)
            got = lax.ppermute(lax.select_n(me, last, first), axis, [(0, 1), (1, 0)])
            zero = jnp.zeros_like(got)
            before = lax.select_n(me, zero, got)
            after = lax.select_n(me, got, zero)
        else:
            up = [(i, (i + 1) % size) for i in range(size - 1)]
            down = [(j, i) for i, j in up]
            before = lax.ppermute(last, axis, up)
            after = lax.ppermute(first, axis, down)
        array = jnp.concatenate([before, array, after], axis=dim)
    return array


def gather_blocks(block, axis):
    size = lax.axis_size(axis)
    me = lax.axis_index(axis)
    got = [block] + [
        lax.ppermute(block, axis, [(j, (j + d) % size) for j in range(size)])
        for d in range(1, size)
    ]
    return jnp.concatenate(
        [lax.select_n((me - j) % size, *got) for j in range(size)], axis=0
    )


def tap_kernel(shifted, active_t, weight_t, slope_x, n_chan, frames, rows):
    _, _, _, cols, outs = shifted.shape
    cells, ins = active_t.shape
    block = ins // n_chan

    def body(cot_ref, act_ref, w_ref, sx_ref, wg_ref, pk_ref, ag_ref):
        act = act_ref[...]
        for kt in range(3):
            for kh in range(3):
                for kw in range(3):
                    k = 9 * kt + 3 * kh + kw
                    piece = cot_ref[kw, 2 - kt : 2 - kt + frames, 2 - kh : 2 - kh + rows]
                    piece = piece.reshape(cells, outs)
                    wg_ref[k] = lax.dot_general(
                        piece, act, (((0,), (0,)), ((), ())),
                        preferred_element_type=jnp.float32,
                    )
                    term = lax.dot_general(
                        w_ref[k], piece, (((1,), (1,)), ((), ())),
                        preferred_element_type=jnp.float32,
                    )
                    if k == 0:
                        ag_ref[...] = term
                    else:
                        ag_ref[...] += term
        ag = ag_ref[...]
        dots = jnp.sum(ag * sx_ref[...], axis=0, keepdims=True)
        for j in range(n_chan):
            pk_ref[j, 0:block, :] = ag[j * block : (j + 1) * block]
            pk_ref[j, block : block + 1, :] = dots

    return pl.pallas_call(
        body,
        out_shape=(
            jax.ShapeDtypeStruct((27, outs, ins), jnp.float32),
            jax.ShapeDtypeStruct((n_chan, block + 1, cells), jnp.float32),
        ),
        in_specs=[pl.BlockSpec(memory_space=pltpu.VMEM)] * 4,
        out_specs=(
            pl.BlockSpec(memory_space=pltpu.VMEM),
            pl.BlockSpec(memory_space=pltpu.VMEM),
        ),
        scratch_shapes=[pltpu.VMEM((ins, cells), jnp.float32)],
        cost_estimate=pl.CostEstimate(
            flops=4 * 27 * ins * cells * outs,
            bytes_accessed=shifted.size * 2 + active_t.size * 2 + weight_t.size * 2
            + slope_x.size * 4 + 27 * ins * outs * 4 + (ins + n_chan) * cells * 4,
            transcendentals=0,
        ),
    )(shifted, active_t, weight_t, slope_x)


def halving_steps(axes):
    steps = []
    for axis in axes:
        size = lax.axis_size(axis)
        idx = lax.axis_index(axis)
        level = 1
        while level < size:
            steps.append((axis, level, (idx // level) % 2))
            level *= 2
    return steps


def exchange(block, axis, level):
    size = lax.axis_size(axis)
    return lax.ppermute(block, axis, [(i, i ^ level) for i in range(size)])


def halving_sum(x, steps):
    for axis, level, bit in steps:
        m = x.shape[0] // 2
        keep = lax.dynamic_slice_in_dim(x, bit * m, m, 0)
        send = lax.dynamic_slice_in_dim(x, (1 - bit) * m, m, 0)
        x = keep + exchange(send, axis, level)
    for axis, level, bit in reversed(steps):
        got = exchange(x, axis, level)
        x = lax.select_n(
            bit, jnp.concatenate([x, got], axis=0), jnp.concatenate([got, x], axis=0)
        )
    return x


def group_sum(x, near, far):
    near_steps, far_steps = halving_steps(near), halving_steps(far)
    unit = 2 ** (len(near_steps) + len(far_steps) + 1)
    rows = x.shape[0]
    padded_rows = -(-rows // unit) * unit
    x = jnp.pad(x, ((0, padded_rows - rows), (0, 0)))
    for axis, level, bit in near_steps:
        m = x.shape[0] // 2
        keep = lax.dynamic_slice_in_dim(x, bit * m, m, 0)
        send = lax.dynamic_slice_in_dim(x, (1 - bit) * m, m, 0)
        x = keep + exchange(send, axis, level)
    half = x.shape[0] // 2
    x = jnp.concatenate(
        [halving_sum(x[:half], far_steps), halving_sum(x[half:], far_steps[::-1])], axis=0
    )
    for axis, level, bit in reversed(near_steps):
        got = exchange(x, axis, level)
        x = lax.select_n(
            bit, jnp.concatenate([x, got], axis=0), jnp.concatenate([got, x], axis=0)
        )
    return x[:rows]


def on_device(features, cotangent, conv_weight, norm_gain, norm_bias):
    chans, frames, rows, cols = features.shape
    n_chan = lax.axis_size("chan")
    whole_x = gather_blocks(features, "chan")
    total = whole_x.shape[0]
    cells = frames * rows * cols
    flat_x = whole_x.reshape(total, cells).astype(jnp.float32)
    inv_rms = lax.rsqrt(jnp.mean(flat_x * flat_x, axis=0, keepdims=True) + 1e-06)
    normed = flat_x * inv_rms * norm_gain[:, None] + norm_bias[:, None]
    active = jax.nn.silu(normed).astype(jnp.bfloat16).reshape(total, frames, rows, cols)

    ahead = from_behind(lax.slice_in_dim(cotangent, 0, 2, axis=1), "tm", -1)
    longer = jnp.concatenate([cotangent, ahead], axis=1)
    bordered = with_halo(longer, (("height", 2),), 1)
    padded = jnp.pad(bordered, ((0, 0), (0, 0), (0, 0), (1, 1)))

    positions = frames * lax.axis_size("tm") * rows * lax.axis_size("height") * cols
    cells_major = jnp.transpose(padded, (1, 2, 3, 0))
    shifted = jnp.stack(
        [cells_major[:, :, 2 - kw : 2 - kw + cols] for kw in range(3)], axis=0
    )
    active_t = jnp.transpose(active.reshape(total, cells))
    sig = jax.nn.sigmoid(normed)
    slope = sig * (1.0 + normed * (1.0 - sig)) * norm_gain[:, None]
    weight_t = jnp.transpose(conv_weight, (1, 2, 0))
    local_sums, packed = tap_kernel(
        shifted, active_t, weight_t, slope * flat_x, n_chan, frames, rows
    )
    summed = group_sum(local_sums.reshape(27 * chans, total), ("height",), ("tm",))
    weight_grad = jnp.transpose(
        (summed / math.sqrt(positions)).reshape(27, chans, total), (1, 0, 2)
    )

    mine = lax.psum_scatter(packed, "chan", scatter_dimension=0, tiled=True)[0]
    act_grad = mine[:chans]
    dots = mine[chans:]

    offset = lax.axis_index("chan") * chans
    own_x = features.reshape(chans, -1).astype(jnp.float32)
    own_slope = lax.dynamic_slice_in_dim(slope, offset, chans, 0)
    upstream = act_grad * own_slope
    own_back = inv_rms * upstream - own_x * inv_rms**3 * dots / total
    result = cotangent.reshape(chans, -1).astype(jnp.float32) + own_back
    return (result.astype(jnp.bfloat16).reshape(features.shape), weight_grad)


def solution(mesh):
    return jax.shard_map(
        on_device,
        mesh=mesh,
        in_specs=(
            P("chan", "tm", "height", None),
            P("chan", "tm", "height", None),
            P("chan", None, None),
            P(),
            P(),
        ),
        out_specs=(P("chan", "tm", "height", None), P("chan", None, None)),
        check_vma=False,
    )
```
